128 devices in a mesh: outer: 4 (over z), inner: 32 (over y, x, core).
Axes of the slice: x: 4, y: 4, z: 4, core: 2. Of those that a mesh axis runs over, the one named last changes fastest.
Arguments:
- tiles: bfloat16 [65536, 128, 128], P(('outer', 'inner')), as said below
- tile_row: int32 [65536], P(('outer', 'inner')), may hold values from 0 to 3, as said below
- tile_col: int32 [65536], P(('outer', 'inner')), may hold values from 0 to 3, as said below
- counts: int32 [16384], P(('outer', 'inner')), may hold values from 1 to 4, as said below
- vectors: bfloat16 [65536, 64], P(('outer', 'inner')), may hold values from -6 to 6
Outputs:
- basis: float32 [65536, 64], P(('outer', 'inner'))
- degree: float32 [65536], P(('outer', 'inner'))
The draws below stay inside these ranges and needn't reach their ends.
Inputs may be any that keep to these rules, and one draw needn't show every extreme that they name: Slot s from sender g to destination h is live exactly when s < counts[g * 128 + h]; the tiles of dead slots hold values that are no part of P. counts is 4 from every sender to itself and 1 to 4 from every sender to every other destination. `tile_row`: A slot from a sender to itself with number s lies in block row s % 4. `tile_col`: A slot from a sender to itself with number s lies in block column s % 4. `tiles`: entries are affinities, zero or positive.
All inputs are finite; a program needn't handle non-finite values.
Results may differ from the reference program's by a relative error of at most 0.004.
Values may be sent and summed in bfloat16 or wider, within the bound.
No kernel may reach another device: no remote copies, remote signals or barrier semaphores. Data moves between devices by JAX's collectives and lax.ppermute only.
A program may use at most 192 MiB of HBM per device.

```python
import math
import jax
import jax.numpy as jnp
from jax import lax

TILE_SIDE = 128
K = 64
SLOTS = 4
DEVICE_ROW_BLOCKS = 4
PEERS = 128
POINTS = 65536
TILE_SLOT_TOTAL = 65536


def draw_tiles(key, part):
    key_value, key_degree_scale = jax.random.split(key, 2)
    array_extent = (TILE_SLOT_TOTAL, TILE_SIDE, TILE_SIDE)
    spread = jax.random.uniform(key_value, array_extent, dtype=jnp.float32)
    row_degree_scale = jnp.exp(jax.random.uniform(key_degree_scale, (TILE_SLOT_TOTAL, TILE_SIDE, 1), dtype=jnp.float32, minval=0.0, maxval=math.log(10.0)))
    values = 3.2 * jnp.exp(-16.0 * spread)
    return (values * row_degree_scale / TILE_SIDE).astype(jnp.bfloat16)


def slot_layout():
    slot_numbers_list = jnp.arange(TILE_SLOT_TOTAL, dtype=jnp.int32)
    sender = slot_numbers_list // (PEERS * SLOTS)
    target = slot_numbers_list // SLOTS % PEERS
    number = slot_numbers_list % SLOTS
    return (sender, target, number)


def draw_tile_row(key, part):
    sender, target, number = slot_layout()
    selected_entries = jax.random.randint(jax.random.fold_in(key, 11), (TILE_SLOT_TOTAL,), 0, DEVICE_ROW_BLOCKS, dtype=jnp.int32)
    return jnp.where(sender == target, number % DEVICE_ROW_BLOCKS, selected_entries).astype(jnp.int32)


def draw_tile_col(key, part):
    sender, target, number = slot_layout()
    selected_entries = jax.random.randint(jax.random.fold_in(key, 12), (TILE_SLOT_TOTAL,), 0, DEVICE_ROW_BLOCKS, dtype=jnp.int32)
    return jnp.where(sender == target, number % DEVICE_ROW_BLOCKS, selected_entries).astype(jnp.int32)


def draw_counts(key, part):
    pair_ids = jnp.arange(PEERS * PEERS, dtype=jnp.int32)
    sender = pair_ids // PEERS
    target = pair_ids % PEERS
    chosen = jax.random.randint(jax.random.fold_in(key, 21), (PEERS * PEERS,), 1, SLOTS + 1, dtype=jnp.int32)
    return jnp.where(sender == target, SLOTS, chosen).astype(jnp.int32)


def block_scale(key, shape, pieces, smallest, high):
    def one(dim, shards_of):
        draws = jax.random.uniform(jax.random.fold_in(jax.random.fold_in(key, 6), dim), (shards_of,), jnp.float32, smallest / len(pieces), high / len(pieces))
        return jnp.repeat(jnp.exp(draws), shape[dim] // shards_of).reshape((-1,) + (1,) * (len(shape) - dim - 1))

    level = one(*pieces[0])
    for cut in pieces[1:]:
        level = level * one(*cut)
    return level


def noise(key, extent, deviation, limit, cuts=(), kind=jnp.bfloat16):
    gain = block_scale(key, extent, cuts, -0.22, 0.18) if cuts else 1.0
    array = jax.random.normal(key, extent, jnp.float32) * deviation * gain
    return jnp.minimum(jnp.maximum(array, -limit), limit).astype(kind)


def setup_inputs(seed: int = 0) -> dict:
    key_list = jax.random.split(jax.random.key(seed), 6)
    tiles = draw_tiles(jax.random.fold_in(key_list[5], 71), 0)
    tile_row = draw_tile_row(jax.random.fold_in(key_list[5], 71), 0)
    tile_col = draw_tile_col(jax.random.fold_in(key_list[5], 71), 0)
    counts = draw_counts(jax.random.fold_in(key_list[5], 71), 0)
    vectors = noise(key_list[4], (POINTS, K), 1.0, 6.0, ((0, 128),))
    return {"tiles": tiles, "tile_row": tile_row, "tile_col": tile_col, "counts": counts, "vectors": vectors}


def reference(tiles, tile_row, tile_col, counts, vectors):
    slot_numbers_list = jnp.arange(TILE_SLOT_TOTAL, dtype=jnp.int32)
    sender = slot_numbers_list // (PEERS * SLOTS)
    target = slot_numbers_list // SLOTS % PEERS
    number = slot_numbers_list % SLOTS
    live = (number < counts[sender * PEERS + target]).astype(jnp.float32)
    row_block = (sender * DEVICE_ROW_BLOCKS + tile_row).astype(jnp.int32)
    col_block = (target * DEVICE_ROW_BLOCKS + tile_col).astype(jnp.int32)
    row_sums = lax.optimization_barrier(jnp.sum(tiles.astype(jnp.float32), axis=2)) * live[:, None]
    col_sums = lax.optimization_barrier(jnp.sum(tiles.astype(jnp.float32), axis=1)) * live[:, None]
    degree_blocks = jnp.zeros((PEERS * DEVICE_ROW_BLOCKS, TILE_SIDE), jnp.float32)
    degree_blocks = degree_blocks.at[row_block].add(row_sums).at[col_block].add(col_sums)
    degree = 1.0 + degree_blocks.reshape(POINTS)
    inv_root = lax.rsqrt(degree)
    scaled = (inv_root[:, None] * vectors.astype(jnp.float32)).astype(jnp.bfloat16)
    scaled_blocks = scaled.astype(jnp.float32).reshape(PEERS * DEVICE_ROW_BLOCKS, TILE_SIDE, K)
    group_tiles = tiles.reshape(PEERS, PEERS * SLOTS, TILE_SIDE, TILE_SIDE)
    group_rows = row_block.reshape(PEERS, PEERS * SLOTS)
    group_cols = col_block.reshape(PEERS, PEERS * SLOTS)
    group_live = live.reshape(PEERS, PEERS * SLOTS)

    def step(total, inputs):
        block_tiles, rows_here, cols_here, live_here = inputs
        dense = block_tiles.astype(jnp.float32)
        forward = jnp.einsum('tab,tbk->tak', dense, scaled_blocks[cols_here])
        mirrored = jnp.einsum('tba,tbk->tak', dense, scaled_blocks[rows_here])
        mirrored = lax.optimization_barrier(mirrored.astype(jnp.bfloat16)).astype(jnp.float32)
        total = total.at[rows_here].add(forward * live_here[:, None, None])
        total = total.at[cols_here].add(mirrored * live_here[:, None, None])
        return (total, None)
    start = jnp.zeros((PEERS * DEVICE_ROW_BLOCKS, TILE_SIDE, K), jnp.float32)
    total, _ = lax.scan(step, start, (group_tiles, group_rows, group_cols, group_live))
    image = inv_root[:, None] * (total.reshape(POINTS, K) + scaled.astype(jnp.float32))
    gram = jnp.dot(image.T, image, precision=lax.Precision.HIGHEST) / jnp.float32(POINTS)
    lower = jnp.linalg.cholesky(gram)
    basis = jax.scipy.linalg.solve_triangular(lower, image.T, lower=True).T
    return (basis, degree)
```

```python
import jax
import jax.numpy as jnp
from jax import lax
from jax.sharding import PartitionSpec as P

AXES = ("outer", "inner")


def butterfly_sum(x, peer_count):
    step = 1
    while step < peer_count:
        perm = [(i, i ^ step) for i in range(peer_count)]
        x = x + lax.ppermute(x, AXES, perm)
        step *= 2
    return x


def shards(tiles, tile_row, tile_col, counts, vectors):
    peer_count = lax.axis_size(AXES)
    outer_count = lax.axis_size("outer")
    inner_count = lax.axis_size("inner")
    slot_total = tiles.shape[0]
    slot_count = slot_total // peer_count
    tile_size = tiles.shape[1]
    rows_dev = vectors.shape[0]
    block_count = rows_dev // tile_size
    vec_width = vectors.shape[1]
    highest = lax.Precision.HIGHEST

    vec_all = lax.all_gather(lax.all_gather(vectors, "outer", axis=0, tiled=True), "inner", axis=0, tiled=True)

    slot_number = jnp.arange(slot_total, dtype=jnp.int32) % slot_count
    live = slot_number < jnp.repeat(counts, slot_count)
    block_ids = jnp.arange(block_count, dtype=jnp.int32)[None, :]
    row_hot = (tile_row[:, None] == block_ids) & live[:, None]
    col_hot = (tile_col[:, None] == block_ids) & live[:, None]

    row_sums = jnp.sum(tiles, axis=2, dtype=jnp.float32)
    col_sums = jnp.sum(tiles, axis=1, dtype=jnp.float32)
    own_part = jnp.einsum("tr,ta->ra", row_hot.astype(jnp.float32), row_sums, precision=highest)
    col_part = jnp.einsum(
        "htr,hta->hra",
        col_hot.astype(jnp.float32).reshape(peer_count, slot_count, block_count),
        col_sums.reshape(peer_count, slot_count, tile_size),
        precision=highest,
    ).reshape(peer_count, block_count * tile_size)
    payload = jnp.concatenate(
        [col_part, tile_col.reshape(peer_count, slot_count).astype(jnp.float32)], axis=1
    )
    got = lax.all_to_all(payload, AXES, split_axis=0, concat_axis=0, tiled=True)
    degree_blocks = own_part + jnp.sum(got[:, : block_count * tile_size], axis=0).reshape(block_count, tile_size)
    got_cols = got[:, block_count * tile_size :].astype(jnp.int32).reshape(peer_count * slot_count)

    degree = 1.0 + degree_blocks.reshape(rows_dev)
    inv_root = lax.rsqrt(degree)
    scaled = (inv_root[:, None] * vectors.astype(jnp.float32)).astype(jnp.bfloat16)

    own_blocks = scaled.reshape(block_count, tile_size, vec_width)
    terms = jnp.einsum(
        "tba,tbk->tak", tiles, own_blocks[tile_row], preferred_element_type=jnp.float32
    ).astype(jnp.bfloat16)
    terms = jnp.where(live[:, None, None], terms, jnp.zeros_like(terms))
    got_terms = lax.all_to_all(terms, AXES, split_axis=0, concat_axis=0, tiled=True)
    got_hot = (got_cols[:, None] == block_ids).astype(jnp.bfloat16)
    mirror = jnp.einsum("tr,tak->rak", got_hot, got_terms, preferred_element_type=jnp.float32)

    inv_all = lax.all_gather(inv_root, AXES, axis=0, tiled=True)
    inv_perm = inv_all.reshape(outer_count, inner_count, rows_dev).transpose(1, 0, 2).reshape(-1)
    scaled_all = (inv_perm[:, None] * vec_all.astype(jnp.float32)).astype(jnp.bfloat16)
    all_blocks = scaled_all.reshape(-1, tile_size, vec_width)
    dest = jnp.arange(slot_total, dtype=jnp.int32) // slot_count
    place = (dest % inner_count) * outer_count + dest // inner_count
    forward = jnp.einsum(
        "tab,tbk->tak", tiles, all_blocks[place * block_count + tile_col], preferred_element_type=jnp.float32
    )
    total = jnp.einsum("tr,tak->rak", row_hot.astype(jnp.float32), forward, precision=highest) + mirror

    image = inv_root[:, None] * (total.reshape(rows_dev, vec_width) + scaled.astype(jnp.float32))
    local_gram = jnp.dot(image.T, image, precision=highest)
    gram = butterfly_sum(local_gram, peer_count) / jnp.float32(rows_dev * peer_count)
    lower = jnp.linalg.cholesky(gram)
    basis = jax.scipy.linalg.solve_triangular(lower, image.T, lower=True).T
    return (basis, degree)


def solution(mesh):
    placed = (
        P(AXES, None, None),
        P(AXES),
        P(AXES),
        P(AXES),
        P(AXES, None),
    )
    return jax.shard_map(
        shards,
        mesh=mesh,
        in_specs=placed,
        out_specs=(P(AXES, None), P(AXES)),
        check_vma=False,
    )
```

```python
import jax
import jax.numpy as jnp
from jax import lax
from jax.sharding import PartitionSpec as P
from jax.experimental import pallas as pl
from jax.experimental.pallas import tpu as pltpu

AXES = ("outer", "inner")


def butterfly_sum(x, peer_count):
    step = 1
    while step < peer_count:
        perm = [(i, i ^ step) for i in range(peer_count)]
        x = x + lax.ppermute(x, AXES, perm)
        step *= 2
    return x


GROUP = 32


def terms_kernel(rows_ref, live_ref, tiles_ref, own_ref, out_ref):
    step = pl.program_id(0)
    size = tiles_ref.shape[1]

    def body(j, carry):
        t = step * GROUP + j
        start = pl.multiple_of(rows_ref[t] * size, size)
        block = own_ref[pl.ds(start, size), :]
        term = lax.dot_general(
            tiles_ref[j], block, (((0,), (0,)), ((), ())), preferred_element_type=jnp.float32
        ).astype(out_ref.dtype)
        out_ref[j] = jnp.where(live_ref[t] > 0, term, jnp.zeros_like(term))
        return carry

    lax.fori_loop(0, GROUP, body, 0)


def mirror_terms(tiles, rows, live, own):
    slots, size, _ = tiles.shape
    width = own.shape[1]
    return pl.pallas_call(
        terms_kernel,
        grid_spec=pltpu.PrefetchScalarGridSpec(
            num_scalar_prefetch=2,
            grid=(slots // GROUP,),
            in_specs=[
                pl.BlockSpec((GROUP, size, size), lambda i, r, l: (i, 0, 0)),
                pl.BlockSpec(memory_space=pltpu.VMEM),
            ],
            out_specs=pl.BlockSpec((GROUP, size, width), lambda i, r, l: (i, 0, 0)),
        ),
        out_shape=jax.ShapeDtypeStruct((slots, size, width), jnp.bfloat16),
    )(rows, live, tiles, own)


def forward_kernel(blocks_ref, rows_ref, live_ref, tiles_ref, all_ref, out_ref):
    step = pl.program_id(0)
    size = tiles_ref.shape[1]

    @pl.when(step == 0)
    def _():
        out_ref[...] = jnp.zeros_like(out_ref)

    def body(j, carry):
        t = step * GROUP + j
        start = pl.multiple_of(blocks_ref[t] * size, size)
        block = all_ref[pl.ds(start, size), :]
        prod = jnp.dot(tiles_ref[j], block, preferred_element_type=jnp.float32)
        r = rows_ref[t]
        out_ref[r] += jnp.where(live_ref[t] > 0, prod, jnp.zeros_like(prod))
        return carry

    lax.fori_loop(0, GROUP, body, 0)


def forward_product(tiles, blocks, rows, live, scaled_all, block_count):
    slots, size, _ = tiles.shape
    width = scaled_all.shape[1]
    return pl.pallas_call(
        forward_kernel,
        grid_spec=pltpu.PrefetchScalarGridSpec(
            num_scalar_prefetch=3,
            grid=(slots // GROUP,),
            in_specs=[
                pl.BlockSpec((GROUP, size, size), lambda i, b, r, l: (i, 0, 0)),
                pl.BlockSpec(memory_space=pltpu.VMEM),
            ],
            out_specs=pl.BlockSpec((block_count, size, width), lambda i, b, r, l: (0, 0, 0)),
        ),
        out_shape=jax.ShapeDtypeStruct((block_count, size, width), jnp.float32),
    )(blocks, rows, live, tiles, scaled_all)


def shards(tiles, tile_row, tile_col, counts, vectors):
    peer_count = lax.axis_size(AXES)
    outer_count = lax.axis_size("outer")
    inner_count = lax.axis_size("inner")
    slot_total = tiles.shape[0]
    slot_count = slot_total // peer_count
    tile_size = tiles.shape[1]
    rows_dev = vectors.shape[0]
    block_count = rows_dev // tile_size
    vec_width = vectors.shape[1]
    highest = lax.Precision.HIGHEST

    vec_all = lax.all_gather(lax.all_gather(vectors, "outer", axis=0, tiled=True), "inner", axis=0, tiled=True)

    slot_number = jnp.arange(slot_total, dtype=jnp.int32) % slot_count
    live = slot_number < jnp.repeat(counts, slot_count)
    block_ids = jnp.arange(block_count, dtype=jnp.int32)[None, :]
    row_hot = (tile_row[:, None] == block_ids) & live[:, None]
    col_hot = (tile_col[:, None] == block_ids) & live[:, None]

    row_sums = jnp.sum(tiles, axis=2, dtype=jnp.float32)
    col_sums = jnp.sum(tiles, axis=1, dtype=jnp.float32)
    own_part = jnp.einsum("tr,ta->ra", row_hot.astype(jnp.float32), row_sums, precision=highest)
    col_part = jnp.einsum(
        "htr,hta->hra",
        col_hot.astype(jnp.float32).reshape(peer_count, slot_count, block_count),
        col_sums.reshape(peer_count, slot_count, tile_size),
        precision=highest,
    ).reshape(peer_count, block_count * tile_size)
    payload = jnp.concatenate(
        [col_part, tile_col.reshape(peer_count, slot_count).astype(jnp.float32)], axis=1
    )
    got = lax.all_to_all(payload, AXES, split_axis=0, concat_axis=0, tiled=True)
    degree_blocks = own_part + jnp.sum(got[:, : block_count * tile_size], axis=0).reshape(block_count, tile_size)
    got_cols = got[:, block_count * tile_size :].astype(jnp.int32).reshape(peer_count * slot_count)

    degree = 1.0 + degree_blocks.reshape(rows_dev)
    inv_root = lax.rsqrt(degree)
    scaled = (inv_root[:, None] * vectors.astype(jnp.float32)).astype(jnp.bfloat16)

    live_i = live.astype(jnp.int32)
    inv_all = lax.all_gather(inv_root, AXES, axis=0, tiled=True)
    terms = mirror_terms(tiles, tile_row, live_i, scaled)
    terms, inv_all = lax.optimization_barrier((terms, inv_all))
    got_terms = lax.all_to_all(terms, AXES, split_axis=0, concat_axis=0, tiled=True)

    inv_perm = inv_all.reshape(outer_count, inner_count, rows_dev).transpose(1, 0, 2).reshape(-1)
    scaled_all = (inv_perm[:, None] * vec_all.astype(jnp.float32)).astype(jnp.bfloat16)
    dest = jnp.arange(slot_total, dtype=jnp.int32) // slot_count
    place = (dest % inner_count) * outer_count + dest // inner_count
    forward = forward_product(tiles, place * block_count + tile_col, tile_row, live_i, scaled_all, block_count)
    forward, got_terms = lax.optimization_barrier((forward, got_terms))
    got_hot = (got_cols[:, None] == block_ids).astype(jnp.bfloat16)
    mirror = jnp.einsum("tr,tak->rak", got_hot, got_terms, preferred_element_type=jnp.float32)
    total = forward + mirror

    image = inv_root[:, None] * (total.reshape(rows_dev, vec_width) + scaled.astype(jnp.float32))
    local_gram = jnp.dot(image.T, image, precision=highest)
    gram = butterfly_sum(local_gram, peer_count) / jnp.float32(rows_dev * peer_count)
    lower = jnp.linalg.cholesky(gram)
    basis = jax.scipy.linalg.solve_triangular(lower, image.T, lower=True).T
    return (basis, degree)


def solution(mesh):
    placed = (
        P(AXES, None, None),
        P(AXES),
        P(AXES),
        P(AXES),
        P(AXES, None),
    )
    return jax.shard_map(
        shards,
        mesh=mesh,
        in_specs=placed,
        out_specs=(P(AXES, None), P(AXES)),
        check_vma=False,
    )
```

```python
import jax
import jax.numpy as jnp
from jax import lax
from jax.sharding import PartitionSpec as P
from jax.experimental import pallas as pl
from jax.experimental.pallas import tpu as pltpu

AXES = ("outer", "inner")


def butterfly_sum(x, peer_count):
    step = 1
    while step < peer_count:
        perm = [(i, i ^ step) for i in range(peer_count)]
        x = x + lax.ppermute(x, AXES, perm)
        step *= 2
    return x


GROUP = 32


def terms_kernel(rows_ref, live_ref, tiles_ref, own_ref, out_ref):
    step = pl.program_id(0)
    size = tiles_ref.shape[1]

    def body(j, carry):
        t = step * GROUP + j
        start = pl.multiple_of(rows_ref[t] * size, size)
        block = own_ref[:, pl.ds(start, size)]
        term = jnp.dot(block, tiles_ref[j], preferred_element_type=jnp.float32).astype(out_ref.dtype)
        out_ref[j] = jnp.where(live_ref[t] > 0, term, jnp.zeros_like(term))
        return carry

    lax.fori_loop(0, GROUP, body, 0, unroll=True)


def mirror_terms(tiles, rows, live, own_t):
    slots, size, _ = tiles.shape
    width = own_t.shape[0]
    return pl.pallas_call(
        terms_kernel,
        grid_spec=pltpu.PrefetchScalarGridSpec(
            num_scalar_prefetch=2,
            grid=(slots // GROUP,),
            in_specs=[
                pl.BlockSpec((GROUP, size, size), lambda i, r, l: (i, 0, 0)),
                pl.BlockSpec(memory_space=pltpu.VMEM),
            ],
            out_specs=pl.BlockSpec((GROUP, width, size), lambda i, r, l: (i, 0, 0)),
        ),
        out_shape=jax.ShapeDtypeStruct((slots, width, size), jnp.bfloat16),
    )(rows, live, tiles, own_t)


def forward_kernel(places_ref, cols_ref, rows_ref, live_ref, tiles_ref, all_ref, out_ref):
    step = pl.program_id(0)
    size = tiles_ref.shape[1]

    @pl.when(step == 0)
    def _():
        out_ref[...] = jnp.zeros_like(out_ref)

    def body(j, carry):
        t = step * GROUP + j
        start = pl.multiple_of(cols_ref[t] * size, size)
        block = all_ref[places_ref[t], :, pl.ds(start, size)]
        prod = lax.dot_general(
            block, tiles_ref[j], (((1,), (1,)), ((), ())), preferred_element_type=jnp.float32
        )
        r = rows_ref[t]
        out_ref[r] += jnp.where(live_ref[t] > 0, prod, jnp.zeros_like(prod))
        return carry

    lax.fori_loop(0, GROUP, body, 0, unroll=True)


def forward_product(tiles, places, cols, rows, live, scaled_all_t, block_count):
    slots, size, _ = tiles.shape
    width = scaled_all_t.shape[1]
    return pl.pallas_call(
        forward_kernel,
        grid_spec=pltpu.PrefetchScalarGridSpec(
            num_scalar_prefetch=4,
            grid=(slots // GROUP,),
            in_specs=[
                pl.BlockSpec((GROUP, size, size), lambda i, p, c, r, l: (i, 0, 0)),
                pl.BlockSpec(memory_space=pltpu.VMEM),
            ],
            out_specs=pl.BlockSpec((block_count, width, size), lambda i, p, c, r, l: (0, 0, 0)),
        ),
        out_shape=jax.ShapeDtypeStruct((block_count, width, size), jnp.float32),
    )(places, cols, rows, live, tiles, scaled_all_t)


def shards(tiles, tile_row, tile_col, counts, vectors):
    peer_count = lax.axis_size(AXES)
    outer_count = lax.axis_size("outer")
    inner_count = lax.axis_size("inner")
    slot_total = tiles.shape[0]
    slot_count = slot_total // peer_count
    tile_size = tiles.shape[1]
    rows_dev = vectors.shape[0]
    block_count = rows_dev // tile_size
    vec_width = vectors.shape[1]
    highest = lax.Precision.HIGHEST

    vec_t = vectors.T
    vec_all = lax.all_gather(lax.all_gather(vec_t, "outer", axis=0), "inner", axis=0)

    slot_number = jnp.arange(slot_total, dtype=jnp.int32) % slot_count
    live = slot_number < jnp.repeat(counts, slot_count)
    block_ids = jnp.arange(block_count, dtype=jnp.int32)[None, :]
    row_hot = (tile_row[:, None] == block_ids) & live[:, None]
    col_hot = (tile_col[:, None] == block_ids) & live[:, None]

    row_sums = jnp.sum(tiles, axis=2, dtype=jnp.float32)
    col_sums = jnp.sum(tiles, axis=1, dtype=jnp.float32)
    own_part = jnp.einsum("tr,ta->ra", row_hot.astype(jnp.float32), row_sums, precision=highest)
    col_part = jnp.einsum(
        "htr,hta->hra",
        col_hot.astype(jnp.float32).reshape(peer_count, slot_count, block_count),
        col_sums.reshape(peer_count, slot_count, tile_size),
        precision=highest,
    ).reshape(peer_count, block_count * tile_size)
    payload = jnp.concatenate(
        [col_part, tile_col.reshape(peer_count, slot_count).astype(jnp.float32)], axis=1
    )
    got = lax.all_to_all(payload, AXES, split_axis=0, concat_axis=0, tiled=True)
    degree_blocks = own_part + jnp.sum(got[:, : block_count * tile_size], axis=0).reshape(block_count, tile_size)
    got_cols = got[:, block_count * tile_size :].astype(jnp.int32).reshape(peer_count * slot_count)

    degree = 1.0 + degree_blocks.reshape(rows_dev)
    inv_root = lax.rsqrt(degree)
    scaled = (inv_root[:, None] * vectors.astype(jnp.float32)).astype(jnp.bfloat16)

    scaled_t = scaled.T
    live_i = live.astype(jnp.int32)
    inv_all = lax.all_gather(inv_root, AXES, axis=0)
    terms = mirror_terms(tiles, tile_row, live_i, scaled_t)
    terms, inv_all = lax.optimization_barrier((terms, inv_all))
    got_terms = lax.all_to_all(terms, AXES, split_axis=0, concat_axis=0, tiled=True)

    inv_perm = inv_all.reshape(outer_count, inner_count, 1, rows_dev).transpose(1, 0, 2, 3)
    scaled_all_t = (inv_perm * vec_all.astype(jnp.float32)).astype(jnp.bfloat16)
    scaled_all_t = scaled_all_t.reshape(peer_count, vec_width, rows_dev)
    dest = jnp.arange(slot_total, dtype=jnp.int32) // slot_count
    place = (dest % inner_count) * outer_count + dest // inner_count
    forward = forward_product(tiles, place, tile_col, tile_row, live_i, scaled_all_t, block_count)
    forward, got_terms = lax.optimization_barrier((forward, got_terms))
    got_hot = (got_cols[:, None] == block_ids).astype(jnp.bfloat16)
    mirror = jnp.einsum("tr,tka->rka", got_hot, got_terms, preferred_element_type=jnp.float32)
    total_t = (forward + mirror).transpose(1, 0, 2).reshape(vec_width, rows_dev)

    image_t = inv_root[None, :] * (total_t + scaled_t.astype(jnp.float32))
    local_gram = jnp.dot(image_t, image_t.T, precision=highest)
    gram = butterfly_sum(local_gram, peer_count) / jnp.float32(rows_dev * peer_count)
    lower = jnp.linalg.cholesky(gram)
    basis = jax.scipy.linalg.solve_triangular(lower, image_t, lower=True).T
    return (basis, degree)


def solution(mesh):
    placed = (
        P(AXES, None, None),
        P(AXES),
        P(AXES),
        P(AXES),
        P(AXES, None),
    )
    return jax.shard_map(
        shards,
        mesh=mesh,
        in_specs=placed,
        out_specs=(P(AXES, None), P(AXES)),
        check_vma=False,
    )
```

```python
import jax
import jax.numpy as jnp
from jax import lax
from jax.sharding import PartitionSpec as P
from jax.experimental import pallas as pl
from jax.experimental.pallas import tpu as pltpu

AXES = ("outer", "inner")


def butterfly_sum(x, peer_count):
    step = 1
    while step < peer_count:
        if step * 4 <= peer_count:
            near = lax.ppermute(x, AXES, [(i, i ^ step) for i in range(peer_count)])
            far = lax.ppermute(x, AXES, [(i, i ^ (2 * step)) for i in range(peer_count)])
            far_near = lax.ppermute(x, AXES, [(i, i ^ (3 * step)) for i in range(peer_count)])
            x = (x + near) + (far + far_near)
            step *= 4
        else:
            x = x + lax.ppermute(x, AXES, [(i, i ^ step) for i in range(peer_count)])
            step *= 2
    return x


GROUP = 32


def terms_kernel(rows_ref, live_ref, tiles_ref, own_ref, out_ref):
    step = pl.program_id(0)
    size = tiles_ref.shape[1]

    def body(j, carry):
        t = step * GROUP + j
        start = pl.multiple_of(rows_ref[t] * size, size)
        block = own_ref[:, pl.ds(start, size)]
        term = jnp.dot(block, tiles_ref[j], preferred_element_type=jnp.float32).astype(out_ref.dtype)
        out_ref[j] = jnp.where(live_ref[t] > 0, term, jnp.zeros_like(term))
        return carry

    lax.fori_loop(0, GROUP, body, 0, unroll=True)


def mirror_terms(tiles, rows, live, own_t):
    slots, size, _ = tiles.shape
    width = own_t.shape[0]
    return pl.pallas_call(
        terms_kernel,
        grid_spec=pltpu.PrefetchScalarGridSpec(
            num_scalar_prefetch=2,
            grid=(slots // GROUP,),
            in_specs=[
                pl.BlockSpec((GROUP, size, size), lambda i, r, l: (i, 0, 0)),
                pl.BlockSpec(memory_space=pltpu.VMEM),
            ],
            out_specs=pl.BlockSpec((GROUP, width, size), lambda i, r, l: (i, 0, 0)),
        ),
        out_shape=jax.ShapeDtypeStruct((slots, width, size), jnp.bfloat16),
    )(rows, live, tiles, own_t)


def forward_kernel(places_ref, cols_ref, rows_ref, live_ref, tiles_ref, all_ref, out_ref):
    step = pl.program_id(0)
    size = tiles_ref.shape[1]

    @pl.when(step == 0)
    def _():
        out_ref[...] = jnp.zeros_like(out_ref)

    def body(j, carry):
        t = step * GROUP + j
        start = pl.multiple_of(cols_ref[t] * size, size)
        block = all_ref[places_ref[t], :, pl.ds(start, size)]
        prod = lax.dot_general(
            block, tiles_ref[j], (((1,), (1,)), ((), ())), preferred_element_type=jnp.float32
        )
        r = rows_ref[t]
        out_ref[r] += jnp.where(live_ref[t] > 0, prod, jnp.zeros_like(prod))
        return carry

    lax.fori_loop(0, GROUP, body, 0, unroll=True)


def forward_product(tiles, places, cols, rows, live, scaled_all_t, block_count):
    slots, size, _ = tiles.shape
    width = scaled_all_t.shape[1]
    return pl.pallas_call(
        forward_kernel,
        grid_spec=pltpu.PrefetchScalarGridSpec(
            num_scalar_prefetch=4,
            grid=(slots // GROUP,),
            in_specs=[
                pl.BlockSpec((GROUP, size, size), lambda i, p, c, r, l: (i, 0, 0)),
                pl.BlockSpec(memory_space=pltpu.VMEM),
            ],
            out_specs=pl.BlockSpec((block_count, width, size), lambda i, p, c, r, l: (0, 0, 0)),
        ),
        out_shape=jax.ShapeDtypeStruct((block_count, width, size), jnp.float32),
    )(places, cols, rows, live, tiles, scaled_all_t)


def shards(tiles, tile_row, tile_col, counts, vectors):
    peer_count = lax.axis_size(AXES)
    outer_count = lax.axis_size("outer")
    inner_count = lax.axis_size("inner")
    slot_total = tiles.shape[0]
    slot_count = slot_total // peer_count
    tile_size = tiles.shape[1]
    rows_dev = vectors.shape[0]
    block_count = rows_dev // tile_size
    vec_width = vectors.shape[1]
    highest = lax.Precision.HIGHEST

    vec_t = vectors.T
    vec_all = lax.all_gather(vec_t, AXES, axis=0)

    slot_number = jnp.arange(slot_total, dtype=jnp.int32) % slot_count
    live = slot_number < jnp.repeat(counts, slot_count)
    block_ids = jnp.arange(block_count, dtype=jnp.int32)[None, :]
    row_hot = (tile_row[:, None] == block_ids) & live[:, None]
    col_hot = (tile_col[:, None] == block_ids) & live[:, None]

    row_sums = jnp.sum(tiles, axis=2, dtype=jnp.float32)
    col_sums = jnp.sum(tiles, axis=1, dtype=jnp.float32)
    own_part = jnp.einsum("tr,ta->ra", row_hot.astype(jnp.float32), row_sums, precision=highest)
    col_part = jnp.einsum(
        "htr,hta->hra",
        col_hot.astype(jnp.float32).reshape(peer_count, slot_count, block_count),
        col_sums.reshape(peer_count, slot_count, tile_size),
        precision=highest,
    ).reshape(peer_count, block_count * tile_size)
    payload = jnp.concatenate(
        [col_part, tile_col.reshape(peer_count, slot_count).astype(jnp.float32)], axis=1
    )
    got = lax.all_to_all(payload, AXES, split_axis=0, concat_axis=0, tiled=True)
    degree_blocks = own_part + jnp.sum(got[:, : block_count * tile_size], axis=0).reshape(block_count, tile_size)
    got_cols = got[:, block_count * tile_size :].astype(jnp.int32).reshape(peer_count * slot_count)

    degree = 1.0 + degree_blocks.reshape(rows_dev)
    inv_root = lax.rsqrt(degree)
    scaled = (inv_root[:, None] * vectors.astype(jnp.float32)).astype(jnp.bfloat16)

    scaled_t = scaled.T
    live_i = live.astype(jnp.int32)
    inv_all = lax.all_gather(inv_root, AXES, axis=0)
    terms = mirror_terms(tiles, tile_row, live_i, scaled_t)
    terms, inv_all = lax.optimization_barrier((terms, inv_all))
    got_terms = lax.all_to_all(terms, AXES, split_axis=0, concat_axis=0, tiled=True)

    scaled_all_t = (inv_all[:, None, :] * vec_all.astype(jnp.float32)).astype(jnp.bfloat16)
    place = jnp.arange(slot_total, dtype=jnp.int32) // slot_count
    forward = forward_product(tiles, place, tile_col, tile_row, live_i, scaled_all_t, block_count)
    forward, got_terms = lax.optimization_barrier((forward, got_terms))
    got_hot = (got_cols[:, None] == block_ids).astype(jnp.bfloat16)
    mirror = jnp.einsum("tr,tka->rka", got_hot, got_terms, preferred_element_type=jnp.float32)
    total_t = (forward + mirror).transpose(1, 0, 2).reshape(vec_width, rows_dev)

    image_t = inv_root[None, :] * (total_t + scaled_t.astype(jnp.float32))
    local_gram = jnp.dot(image_t, image_t.T, precision=highest)
    gram = butterfly_sum(local_gram, peer_count) / jnp.float32(rows_dev * peer_count)
    lower = jnp.linalg.cholesky(gram)
    basis = jax.scipy.linalg.solve_triangular(lower, image_t, lower=True).T
    return (basis, degree)


def solution(mesh):
    placed = (
        P(AXES, None, None),
        P(AXES),
        P(AXES),
        P(AXES),
        P(AXES, None),
    )
    return jax.shard_map(
        shards,
        mesh=mesh,
        in_specs=placed,
        out_specs=(P(AXES, None), P(AXES)),
        check_vma=False,
    )
```

```python
import jax
import jax.numpy as jnp
from jax import lax
from jax.sharding import PartitionSpec as P
from jax.experimental import pallas as pl
from jax.experimental.pallas import tpu as pltpu

AXES = ("outer", "inner")


def butterfly_sum(x, peer_count):
    step = 1
    while step < peer_count:
        if step * 4 <= peer_count:
            near = lax.ppermute(x, AXES, [(i, i ^ step) for i in range(peer_count)])
            far = lax.ppermute(x, AXES, [(i, i ^ (2 * step)) for i in range(peer_count)])
            far_near = lax.ppermute(x, AXES, [(i, i ^ (3 * step)) for i in range(peer_count)])
            x = (x + near) + (far + far_near)
            step *= 4
        else:
            x = x + lax.ppermute(x, AXES, [(i, i ^ step) for i in range(peer_count)])
            step *= 2
    return x


GROUP = 32


def terms_kernel(rows_ref, live_ref, tiles_ref, own_ref, out_ref):
    step = pl.program_id(0)
    size = tiles_ref.shape[1]

    def body(j, carry):
        t = step * GROUP + j
        start = pl.multiple_of(rows_ref[t] * size, size)
        block = own_ref[:, pl.ds(start, size)]
        term = jnp.dot(block, tiles_ref[j], preferred_element_type=jnp.float32).astype(out_ref.dtype)
        out_ref[j] = jnp.where(live_ref[t] > 0, term, jnp.zeros_like(term))
        return carry

    lax.fori_loop(0, GROUP, body, 0, unroll=True)


def mirror_terms(tiles, rows, live, own_t):
    slots, size, _ = tiles.shape
    width = own_t.shape[0]
    return pl.pallas_call(
        terms_kernel,
        grid_spec=pltpu.PrefetchScalarGridSpec(
            num_scalar_prefetch=2,
            grid=(slots // GROUP,),
            in_specs=[
                pl.BlockSpec((GROUP, size, size), lambda i, r, l: (i, 0, 0)),
                pl.BlockSpec(memory_space=pltpu.VMEM),
            ],
            out_specs=pl.BlockSpec((GROUP, width, size), lambda i, r, l: (i, 0, 0)),
        ),
        out_shape=jax.ShapeDtypeStruct((slots, width, size), jnp.bfloat16),
    )(rows, live, tiles, own_t)


def forward_kernel(places_ref, cols_ref, rows_ref, live_ref, tiles_ref, all_ref, out_ref):
    step = pl.program_id(0)
    size = tiles_ref.shape[1]

    @pl.when(step == 0)
    def _():
        out_ref[...] = jnp.zeros_like(out_ref)

    def body(j, carry):
        t = step * GROUP + j
        start = pl.multiple_of(cols_ref[t] * size, size)
        block = all_ref[places_ref[t], :, pl.ds(start, size)]
        prod = lax.dot_general(
            block, tiles_ref[j], (((1,), (1,)), ((), ())), preferred_element_type=jnp.float32
        )
        r = rows_ref[t]
        out_ref[r] += jnp.where(live_ref[t] > 0, prod, jnp.zeros_like(prod))
        return carry

    lax.fori_loop(0, GROUP, body, 0, unroll=True)


def forward_product(tiles, places, cols, rows, live, scaled_all_t, block_count):
    slots, size, _ = tiles.shape
    width = scaled_all_t.shape[1]
    return pl.pallas_call(
        forward_kernel,
        grid_spec=pltpu.PrefetchScalarGridSpec(
            num_scalar_prefetch=4,
            grid=(slots // GROUP,),
            in_specs=[
                pl.BlockSpec((GROUP, size, size), lambda i, p, c, r, l: (i, 0, 0)),
                pl.BlockSpec(memory_space=pltpu.VMEM),
            ],
            out_specs=pl.BlockSpec((block_count, width, size), lambda i, p, c, r, l: (0, 0, 0)),
        ),
        out_shape=jax.ShapeDtypeStruct((block_count, width, size), jnp.float32),
    )(places, cols, rows, live, tiles, scaled_all_t)


def shards(tiles, tile_row, tile_col, counts, vectors):
    peer_count = lax.axis_size(AXES)
    outer_count = lax.axis_size("outer")
    inner_count = lax.axis_size("inner")
    slot_total = tiles.shape[0]
    slot_count = slot_total // peer_count
    tile_size = tiles.shape[1]
    rows_dev = vectors.shape[0]
    block_count = rows_dev // tile_size
    vec_width = vectors.shape[1]
    highest = lax.Precision.HIGHEST

    vec_t = vectors.T
    vec_all = lax.all_gather(vec_t, AXES, axis=0)

    slot_number = jnp.arange(slot_total, dtype=jnp.int32) % slot_count
    live = slot_number < jnp.repeat(counts, slot_count)
    block_ids = jnp.arange(block_count, dtype=jnp.int32)[None, :]
    row_hot = (tile_row[:, None] == block_ids) & live[:, None]
    col_hot = (tile_col[:, None] == block_ids) & live[:, None]

    row_sums = jnp.sum(tiles, axis=2, dtype=jnp.float32)
    col_sums = jnp.sum(tiles, axis=1, dtype=jnp.float32)
    own_part = jnp.einsum("tr,ta->ra", row_hot.astype(jnp.float32), row_sums, precision=highest)
    col_part = jnp.einsum(
        "htr,hta->hra",
        col_hot.astype(jnp.float32).reshape(peer_count, slot_count, block_count),
        col_sums.reshape(peer_count, slot_count, tile_size),
        precision=highest,
    ).reshape(peer_count, block_count * tile_size)
    payload = jnp.concatenate(
        [col_part, tile_col.reshape(peer_count, slot_count).astype(jnp.float32)], axis=1
    )
    got = lax.all_to_all(payload, AXES, split_axis=0, concat_axis=0, tiled=True)
    degree_blocks = own_part + jnp.sum(got[:, : block_count * tile_size], axis=0).reshape(block_count, tile_size)
    got_cols = got[:, block_count * tile_size :].astype(jnp.int32).reshape(peer_count * slot_count)

    degree = 1.0 + degree_blocks.reshape(rows_dev)
    inv_root = lax.rsqrt(degree)
    scaled = (inv_root[:, None] * vectors.astype(jnp.float32)).astype(jnp.bfloat16)

    scaled_t = scaled.T
    live_i = live.astype(jnp.int32)
    inv_rows, vec_all = lax.optimization_barrier((jnp.broadcast_to(inv_root[None, :], (8, rows_dev)), vec_all))
    inv_all = lax.all_gather(inv_rows, AXES, axis=0)[:, 0, :]
    terms = mirror_terms(tiles, tile_row, live_i, scaled_t)
    got_terms = lax.all_to_all(terms, AXES, split_axis=0, concat_axis=0, tiled=True)

    scaled_all_t = (inv_all[:, None, :] * vec_all.astype(jnp.float32)).astype(jnp.bfloat16)
    place = jnp.arange(slot_total, dtype=jnp.int32) // slot_count
    forward = forward_product(tiles, place, tile_col, tile_row, live_i, scaled_all_t, block_count)
    forward, got_terms = lax.optimization_barrier((forward, got_terms))
    got_hot = (got_cols[:, None] == block_ids).astype(jnp.bfloat16)
    mirror = jnp.einsum("tr,tka->rka", got_hot, got_terms, preferred_element_type=jnp.float32)
    total_t = (forward + mirror).transpose(1, 0, 2).reshape(vec_width, rows_dev)

    image_t = inv_root[None, :] * (total_t + scaled_t.astype(jnp.float32))
    local_gram = jnp.dot(image_t, image_t.T, precision=highest)
    gram = butterfly_sum(local_gram, peer_count) / jnp.float32(rows_dev * peer_count)
    lower = jnp.linalg.cholesky(gram)
    basis = jax.scipy.linalg.solve_triangular(lower, image_t, lower=True).T
    return (basis, degree)


def solution(mesh):
    placed = (
        P(AXES, None, None),
        P(AXES),
        P(AXES),
        P(AXES),
        P(AXES, None),
    )
    return jax.shard_map(
        shards,
        mesh=mesh,
        in_specs=placed,
        out_specs=(P(AXES, None), P(AXES)),
        check_vma=False,
    )
```

```python
import jax
import jax.numpy as jnp
from jax import lax
from jax.sharding import PartitionSpec as P
from jax.experimental import pallas as pl
from jax.experimental.pallas import tpu as pltpu

AXES = ("outer", "inner")


def butterfly_sum(x, peer_count):
    step = 1
    while step < peer_count:
        if step * 4 <= peer_count:
            near = lax.ppermute(x, AXES, [(i, i ^ step) for i in range(peer_count)])
            far = lax.ppermute(x, AXES, [(i, i ^ (2 * step)) for i in range(peer_count)])
            far_near = lax.ppermute(x, AXES, [(i, i ^ (3 * step)) for i in range(peer_count)])
            x = (x + near) + (far + far_near)
            step *= 4
        else:
            x = x + lax.ppermute(x, AXES, [(i, i ^ step) for i in range(peer_count)])
            step *= 2
    return x


GROUP = 32


def terms_kernel(rows_ref, live_ref, tiles_ref, own_ref, out_ref):
    step = pl.program_id(0)
    size = tiles_ref.shape[1]

    def body(j, carry):
        t = step * GROUP + j
        start = pl.multiple_of(rows_ref[t] * size, size)
        block = own_ref[:, pl.ds(start, size)]
        term = jnp.dot(block, tiles_ref[j], preferred_element_type=jnp.float32).astype(out_ref.dtype)
        out_ref[j] = jnp.where(live_ref[t] > 0, term, jnp.zeros_like(term))
        return carry

    lax.fori_loop(0, GROUP, body, 0, unroll=True)


def mirror_terms(tiles, rows, live, own_t):
    slots, size, _ = tiles.shape
    width = own_t.shape[0]
    return pl.pallas_call(
        terms_kernel,
        grid_spec=pltpu.PrefetchScalarGridSpec(
            num_scalar_prefetch=2,
            grid=(slots // GROUP,),
            in_specs=[
                pl.BlockSpec((GROUP, size, size), lambda i, r, l: (i, 0, 0)),
                pl.BlockSpec(memory_space=pltpu.VMEM),
            ],
            out_specs=pl.BlockSpec((GROUP, width, size), lambda i, r, l: (i, 0, 0)),
        ),
        out_shape=jax.ShapeDtypeStruct((slots, width, size), jnp.bfloat16),
    )(rows, live, tiles, own_t)


def forward_kernel(places_ref, cols_ref, rows_ref, live_ref, tiles_ref, all_ref, out_ref):
    step = pl.program_id(0)
    size = tiles_ref.shape[1]

    @pl.when(step == 0)
    def _():
        out_ref[...] = jnp.zeros_like(out_ref)

    def body(j, carry):
        t = step * GROUP + j
        start = pl.multiple_of(cols_ref[t] * size, size)
        block = all_ref[places_ref[t], :, pl.ds(start, size)]
        prod = lax.dot_general(
            block, tiles_ref[j], (((1,), (1,)), ((), ())), preferred_element_type=jnp.float32
        )
        r = rows_ref[t]
        out_ref[r] += jnp.where(live_ref[t] > 0, prod, jnp.zeros_like(prod))
        return carry

    lax.fori_loop(0, GROUP, body, 0, unroll=True)


def forward_product(tiles, places, cols, rows, live, scaled_all_t, block_count):
    slots, size, _ = tiles.shape
    width = scaled_all_t.shape[1]
    return pl.pallas_call(
        forward_kernel,
        grid_spec=pltpu.PrefetchScalarGridSpec(
            num_scalar_prefetch=4,
            grid=(slots // GROUP,),
            in_specs=[
                pl.BlockSpec((GROUP, size, size), lambda i, p, c, r, l: (i, 0, 0)),
                pl.BlockSpec(memory_space=pltpu.VMEM),
            ],
            out_specs=pl.BlockSpec((block_count, width, size), lambda i, p, c, r, l: (0, 0, 0)),
        ),
        out_shape=jax.ShapeDtypeStruct((block_count, width, size), jnp.float32),
    )(places, cols, rows, live, tiles, scaled_all_t)


def shards(tiles, tile_row, tile_col, counts, vectors):
    peer_count = lax.axis_size(AXES)
    outer_count = lax.axis_size("outer")
    inner_count = lax.axis_size("inner")
    slot_total = tiles.shape[0]
    slot_count = slot_total // peer_count
    tile_size = tiles.shape[1]
    rows_dev = vectors.shape[0]
    block_count = rows_dev // tile_size
    vec_width = vectors.shape[1]
    highest = lax.Precision.HIGHEST

    vec_t = vectors.T
    vec_all = lax.all_gather(vec_t, AXES, axis=0)

    slot_number = jnp.arange(slot_total, dtype=jnp.int32) % slot_count
    live = slot_number < jnp.repeat(counts, slot_count)
    block_ids = jnp.arange(block_count, dtype=jnp.int32)[None, :]
    row_hot = (tile_row[:, None] == block_ids) & live[:, None]
    col_hot = (tile_col[:, None] == block_ids) & live[:, None]

    row_sums = jnp.sum(tiles, axis=2, dtype=jnp.float32)
    col_sums = jnp.sum(tiles, axis=1, dtype=jnp.float32)
    own_part = jnp.einsum("tr,ta->ra", row_hot.astype(jnp.float32), row_sums, precision=highest)
    col_part = jnp.einsum(
        "htr,hta->hra",
        col_hot.astype(jnp.float32).reshape(peer_count, slot_count, block_count),
        col_sums.reshape(peer_count, slot_count, tile_size),
        precision=highest,
    ).reshape(peer_count, block_count * tile_size)
    payload = jnp.concatenate(
        [col_part, tile_col.reshape(peer_count, slot_count).astype(jnp.float32)], axis=1
    )
    got = lax.all_to_all(payload, AXES, split_axis=0, concat_axis=0, tiled=True)
    degree_blocks = own_part + jnp.sum(got[:, : block_count * tile_size], axis=0).reshape(block_count, tile_size)
    got_cols = got[:, block_count * tile_size :].astype(jnp.int32).reshape(peer_count * slot_count)

    degree = 1.0 + degree_blocks.reshape(rows_dev)
    inv_root = lax.rsqrt(degree)
    scaled = (inv_root[:, None] * vectors.astype(jnp.float32)).astype(jnp.bfloat16)

    scaled_t = scaled.T
    live_i = live.astype(jnp.int32)
    inv_all = lax.all_to_all(
        jnp.broadcast_to(inv_root[None, :], (peer_count, rows_dev)), AXES, split_axis=0, concat_axis=0, tiled=True
    )
    terms = mirror_terms(tiles, tile_row, live_i, scaled_t)
    terms, inv_all = lax.optimization_barrier((terms, inv_all))
    got_terms = lax.all_to_all(terms, AXES, split_axis=0, concat_axis=0, tiled=True)

    scaled_all_t = (inv_all[:, None, :] * vec_all.astype(jnp.float32)).astype(jnp.bfloat16)
    place = jnp.arange(slot_total, dtype=jnp.int32) // slot_count
    forward = forward_product(tiles, place, tile_col, tile_row, live_i, scaled_all_t, block_count)
    forward, got_terms = lax.optimization_barrier((forward, got_terms))
    got_hot = (got_cols[:, None] == block_ids).astype(jnp.bfloat16)
    mirror = jnp.einsum("tr,tka->rka", got_hot, got_terms, preferred_element_type=jnp.float32)
    total_t = (forward + mirror).transpose(1, 0, 2).reshape(vec_width, rows_dev)

    image_t = inv_root[None, :] * (total_t + scaled_t.astype(jnp.float32))
    local_gram = jnp.dot(image_t, image_t.T, precision=highest)
    gram = butterfly_sum(local_gram, peer_count) / jnp.float32(rows_dev * peer_count)
    lower = jnp.linalg.cholesky(gram)
    basis = jax.scipy.linalg.solve_triangular(lower, image_t, lower=True).T
    return (basis, degree)


def solution(mesh):
    placed = (
        P(AXES, None, None),
        P(AXES),
        P(AXES),
        P(AXES),
        P(AXES, None),
    )
    return jax.shard_map(
        shards,
        mesh=mesh,
        in_specs=placed,
        out_specs=(P(AXES, None), P(AXES)),
        check_vma=False,
    )
```

```python
import jax
import jax.numpy as jnp
from jax import lax
from jax.sharding import PartitionSpec as P
from jax.experimental import pallas as pl
from jax.experimental.pallas import tpu as pltpu

AXES = ("outer", "inner")


def butterfly_sum(x, peer_count):
    step = 1
    while step < peer_count:
        if step * 4 <= peer_count:
            near = lax.ppermute(x, AXES, [(i, i ^ step) for i in range(peer_count)])
            far = lax.ppermute(x, AXES, [(i, i ^ (2 * step)) for i in range(peer_count)])
            far_near = lax.ppermute(x, AXES, [(i, i ^ (3 * step)) for i in range(peer_count)])
            x = (x + near) + (far + far_near)
            step *= 4
        else:
            x = x + lax.ppermute(x, AXES, [(i, i ^ step) for i in range(peer_count)])
            step *= 2
    return x


GROUP = 32


def terms_kernel(rows_ref, live_ref, tiles_ref, own_ref, out_ref):
    step = pl.program_id(0)
    size = tiles_ref.shape[1]

    def body(j, carry):
        t = step * GROUP + j
        start = pl.multiple_of(rows_ref[t] * size, size)
        block = own_ref[:, pl.ds(start, size)]
        term = jnp.dot(block, tiles_ref[j], preferred_element_type=jnp.float32).astype(out_ref.dtype)
        out_ref[j] = jnp.where(live_ref[t] > 0, term, jnp.zeros_like(term))
        return carry

    lax.fori_loop(0, GROUP, body, 0, unroll=True)


def mirror_terms(tiles, rows, live, own_t):
    slots, size, _ = tiles.shape
    width = own_t.shape[0]
    return pl.pallas_call(
        terms_kernel,
        grid_spec=pltpu.PrefetchScalarGridSpec(
            num_scalar_prefetch=2,
            grid=(slots // GROUP,),
            in_specs=[
                pl.BlockSpec((GROUP, size, size), lambda i, r, l: (i, 0, 0)),
                pl.BlockSpec(memory_space=pltpu.VMEM),
            ],
            out_specs=pl.BlockSpec((GROUP, width, size), lambda i, r, l: (i, 0, 0)),
        ),
        out_shape=jax.ShapeDtypeStruct((slots, width, size), jnp.bfloat16),
    )(rows, live, tiles, own_t)


def forward_kernel(places_ref, cols_ref, rows_ref, live_ref, tiles_ref, all_ref, out_ref):
    step = pl.program_id(0)
    size = tiles_ref.shape[1]

    @pl.when(step == 0)
    def _():
        out_ref[...] = jnp.zeros_like(out_ref)

    def body(j, carry):
        t = step * GROUP + j
        start = pl.multiple_of(cols_ref[t] * size, size)
        block = all_ref[places_ref[t], :, pl.ds(start, size)]
        prod = lax.dot_general(
            block, tiles_ref[j], (((1,), (1,)), ((), ())), preferred_element_type=jnp.float32
        )
        r = rows_ref[t]
        out_ref[r] += jnp.where(live_ref[t] > 0, prod, jnp.zeros_like(prod))
        return carry

    lax.fori_loop(0, GROUP, body, 0, unroll=True)


def forward_product(tiles, places, cols, rows, live, scaled_all_t, block_count):
    slots, size, _ = tiles.shape
    width = scaled_all_t.shape[1]
    return pl.pallas_call(
        forward_kernel,
        grid_spec=pltpu.PrefetchScalarGridSpec(
            num_scalar_prefetch=4,
            grid=(slots // GROUP,),
            in_specs=[
                pl.BlockSpec((GROUP, size, size), lambda i, p, c, r, l: (i, 0, 0)),
                pl.BlockSpec(memory_space=pltpu.VMEM),
            ],
            out_specs=pl.BlockSpec((block_count, width, size), lambda i, p, c, r, l: (0, 0, 0)),
        ),
        out_shape=jax.ShapeDtypeStruct((block_count, width, size), jnp.float32),
    )(places, cols, rows, live, tiles, scaled_all_t)


MIRROR_GROUP = 64


def mirror_kernel(cols_ref, got_ref, out_ref):
    step = pl.program_id(0)

    @pl.when(step == 0)
    def _():
        out_ref[...] = jnp.zeros_like(out_ref)

    def body(j, carry):
        c = cols_ref[step * MIRROR_GROUP + j]
        out_ref[c] += got_ref[j].astype(jnp.float32)
        return carry

    lax.fori_loop(0, MIRROR_GROUP, body, 0, unroll=True)


def mirror_sum(cols, got_terms, block_count):
    slots, width, size = got_terms.shape
    return pl.pallas_call(
        mirror_kernel,
        grid_spec=pltpu.PrefetchScalarGridSpec(
            num_scalar_prefetch=1,
            grid=(slots // MIRROR_GROUP,),
            in_specs=[pl.BlockSpec((MIRROR_GROUP, width, size), lambda i, c: (i, 0, 0))],
            out_specs=pl.BlockSpec((block_count, width, size), lambda i, c: (0, 0, 0)),
        ),
        out_shape=jax.ShapeDtypeStruct((block_count, width, size), jnp.float32),
    )(cols, got_terms)


def shards(tiles, tile_row, tile_col, counts, vectors):
    peer_count = lax.axis_size(AXES)
    outer_count = lax.axis_size("outer")
    inner_count = lax.axis_size("inner")
    slot_total = tiles.shape[0]
    slot_count = slot_total // peer_count
    tile_size = tiles.shape[1]
    rows_dev = vectors.shape[0]
    block_count = rows_dev // tile_size
    vec_width = vectors.shape[1]
    highest = lax.Precision.HIGHEST

    vec_t = vectors.T
    vec_all = lax.all_gather(vec_t, AXES, axis=0)

    slot_number = jnp.arange(slot_total, dtype=jnp.int32) % slot_count
    live = slot_number < jnp.repeat(counts, slot_count)
    block_ids = jnp.arange(block_count, dtype=jnp.int32)[None, :]
    row_hot = (tile_row[:, None] == block_ids) & live[:, None]
    col_hot = (tile_col[:, None] == block_ids) & live[:, None]

    row_sums = jnp.sum(tiles, axis=2, dtype=jnp.float32)
    col_sums = jnp.sum(tiles, axis=1, dtype=jnp.float32)
    own_part = jnp.einsum("tr,ta->ra", row_hot.astype(jnp.float32), row_sums, precision=highest)
    col_part = jnp.einsum(
        "htr,hta->hra",
        col_hot.astype(jnp.float32).reshape(peer_count, slot_count, block_count),
        col_sums.reshape(peer_count, slot_count, tile_size),
        precision=highest,
    ).reshape(peer_count, block_count * tile_size)
    payload = jnp.concatenate(
        [col_part, tile_col.reshape(peer_count, slot_count).astype(jnp.float32)], axis=1
    )
    got = lax.all_to_all(payload, AXES, split_axis=0, concat_axis=0, tiled=True)
    degree_blocks = own_part + jnp.sum(got[:, : block_count * tile_size], axis=0).reshape(block_count, tile_size)
    got_cols = got[:, block_count * tile_size :].astype(jnp.int32).reshape(peer_count * slot_count)

    degree = 1.0 + degree_blocks.reshape(rows_dev)
    inv_root = lax.rsqrt(degree)
    scaled = (inv_root[:, None] * vectors.astype(jnp.float32)).astype(jnp.bfloat16)

    scaled_t = scaled.T
    live_i = live.astype(jnp.int32)
    inv_all = lax.all_to_all(
        jnp.broadcast_to(inv_root[None, :], (peer_count, rows_dev)), AXES, split_axis=0, concat_axis=0, tiled=True
    )
    terms = mirror_terms(tiles, jnp.clip(tile_row, 0, block_count - 1), live_i, scaled_t)
    terms, inv_all = lax.optimization_barrier((terms, inv_all))
    got_terms = lax.all_to_all(terms, AXES, split_axis=0, concat_axis=0, tiled=True)

    scaled_all_t = (inv_all[:, None, :] * vec_all.astype(jnp.float32)).astype(jnp.bfloat16)
    place = jnp.arange(slot_total, dtype=jnp.int32) // slot_count
    row_idx = jnp.clip(tile_row, 0, block_count - 1)
    col_idx = jnp.clip(tile_col, 0, block_count - 1)
    forward = forward_product(tiles, place, col_idx, row_idx, live_i, scaled_all_t, block_count)
    forward, got_terms = lax.optimization_barrier((forward, got_terms))
    mirror = mirror_sum(jnp.clip(got_cols, 0, block_count - 1), got_terms, block_count)
    total_t = (forward + mirror).transpose(1, 0, 2).reshape(vec_width, rows_dev)

    image_t = inv_root[None, :] * (total_t + scaled_t.astype(jnp.float32))
    local_gram = jnp.dot(image_t, image_t.T, precision=highest)
    gram = butterfly_sum(local_gram, peer_count) / jnp.float32(rows_dev * peer_count)
    lower = jnp.linalg.cholesky(gram)
    basis = jax.scipy.linalg.solve_triangular(lower, image_t, lower=True).T
    return (basis, degree)


def solution(mesh):
    placed = (
        P(AXES, None, None),
        P(AXES),
        P(AXES),
        P(AXES),
        P(AXES, None),
    )
    return jax.shard_map(
        shards,
        mesh=mesh,
        in_specs=placed,
        out_specs=(P(AXES, None), P(AXES)),
        check_vma=False,
    )
```

```python
import jax
import jax.numpy as jnp
from jax import lax
from jax.sharding import PartitionSpec as P
from jax.experimental import pallas as pl
from jax.experimental.pallas import tpu as pltpu

AXES = ("outer", "inner")


def butterfly_sum(x, peer_count):
    step = 1
    while step < peer_count:
        if step * 4 <= peer_count:
            near = lax.ppermute(x, AXES, [(i, i ^ step) for i in range(peer_count)])
            far = lax.ppermute(x, AXES, [(i, i ^ (2 * step)) for i in range(peer_count)])
            far_near = lax.ppermute(x, AXES, [(i, i ^ (3 * step)) for i in range(peer_count)])
            x = (x + near) + (far + far_near)
            step *= 4
        else:
            x = x + lax.ppermute(x, AXES, [(i, i ^ step) for i in range(peer_count)])
            step *= 2
    return x


GROUP = 32


TERMS_GROUP = 256


def terms_kernel(rows_ref, live_ref, tiles_ref, own_ref, out_ref):
    step = pl.program_id(0)
    size = tiles_ref.shape[1]

    for j in range(TERMS_GROUP):
        t = step * TERMS_GROUP + j
        start = pl.multiple_of(rows_ref[t] * size, size)
        block = own_ref[:, pl.ds(start, size)]
        term = jnp.dot(block, tiles_ref[j], preferred_element_type=jnp.float32).astype(out_ref.dtype)
        out_ref[j] = jnp.where(live_ref[t] > 0, term, jnp.zeros_like(term))


def mirror_terms(tiles, rows, live, own_t):
    slots, size, _ = tiles.shape
    width = own_t.shape[0]
    return pl.pallas_call(
        terms_kernel,
        grid_spec=pltpu.PrefetchScalarGridSpec(
            num_scalar_prefetch=2,
            grid=(slots // TERMS_GROUP,),
            in_specs=[
                pl.BlockSpec((TERMS_GROUP, size, size), lambda i, r, l: (i, 0, 0)),
                pl.BlockSpec(memory_space=pltpu.VMEM),
            ],
            out_specs=pl.BlockSpec((TERMS_GROUP, width, size), lambda i, r, l: (i, 0, 0)),
        ),
        out_shape=jax.ShapeDtypeStruct((slots, width, size), jnp.bfloat16),
    )(rows, live, tiles, own_t)


def forward_kernel(places_ref, cols_ref, rows_ref, live_ref, tiles_ref, all_ref, out_ref):
    step = pl.program_id(0)
    size = tiles_ref.shape[1]

    @pl.when(step == 0)
    def _():
        out_ref[...] = jnp.zeros_like(out_ref)

    def body(j, carry):
        t = step * GROUP + j
        start = pl.multiple_of(cols_ref[t] * size, size)
        block = all_ref[places_ref[t], :, pl.ds(start, size)]
        prod = lax.dot_general(
            block, tiles_ref[j], (((1,), (1,)), ((), ())), preferred_element_type=jnp.float32
        )
        r = rows_ref[t]
        out_ref[r] += jnp.where(live_ref[t] > 0, prod, jnp.zeros_like(prod))
        return carry

    lax.fori_loop(0, GROUP, body, 0, unroll=True)


def forward_product(tiles, places, cols, rows, live, scaled_all_t, block_count):
    slots, size, _ = tiles.shape
    width = scaled_all_t.shape[1]
    return pl.pallas_call(
        forward_kernel,
        grid_spec=pltpu.PrefetchScalarGridSpec(
            num_scalar_prefetch=4,
            grid=(slots // GROUP,),
            in_specs=[
                pl.BlockSpec((GROUP, size, size), lambda i, p, c, r, l: (i, 0, 0)),
                pl.BlockSpec(memory_space=pltpu.VMEM),
            ],
            out_specs=pl.BlockSpec((block_count, width, size), lambda i, p, c, r, l: (0, 0, 0)),
        ),
        out_shape=jax.ShapeDtypeStruct((block_count, width, size), jnp.float32),
    )(places, cols, rows, live, tiles, scaled_all_t)


def shards(tiles, tile_row, tile_col, counts, vectors):
    peer_count = lax.axis_size(AXES)
    outer_count = lax.axis_size("outer")
    inner_count = lax.axis_size("inner")
    slot_total = tiles.shape[0]
    slot_count = slot_total // peer_count
    tile_size = tiles.shape[1]
    rows_dev = vectors.shape[0]
    block_count = rows_dev // tile_size
    vec_width = vectors.shape[1]
    highest = lax.Precision.HIGHEST

    vec_t = vectors.T
    vec_all = lax.all_gather(vec_t, AXES, axis=0)

    slot_number = jnp.arange(slot_total, dtype=jnp.int32) % slot_count
    live = slot_number < jnp.repeat(counts, slot_count)
    block_ids = jnp.arange(block_count, dtype=jnp.int32)[None, :]
    row_hot = (tile_row[:, None] == block_ids) & live[:, None]
    col_hot = (tile_col[:, None] == block_ids) & live[:, None]

    row_sums = jnp.sum(tiles, axis=2, dtype=jnp.float32)
    col_sums = jnp.sum(tiles, axis=1, dtype=jnp.float32)
    own_part = jnp.einsum("tr,ta->ra", row_hot.astype(jnp.float32), row_sums, precision=highest)
    col_part = jnp.einsum(
        "htr,hta->hra",
        col_hot.astype(jnp.float32).reshape(peer_count, slot_count, block_count),
        col_sums.reshape(peer_count, slot_count, tile_size),
        precision=highest,
    ).reshape(peer_count, block_count * tile_size)
    payload = jnp.concatenate(
        [col_part, tile_col.reshape(peer_count, slot_count).astype(jnp.float32)], axis=1
    )
    got = lax.all_to_all(payload, AXES, split_axis=0, concat_axis=0, tiled=True)
    degree_blocks = own_part + jnp.sum(got[:, : block_count * tile_size], axis=0).reshape(block_count, tile_size)
    got_cols = got[:, block_count * tile_size :].astype(jnp.int32).reshape(peer_count * slot_count)

    degree = 1.0 + degree_blocks.reshape(rows_dev)
    inv_root = lax.rsqrt(degree)
    scaled = (inv_root[:, None] * vectors.astype(jnp.float32)).astype(jnp.bfloat16)

    scaled_t = scaled.T
    live_i = live.astype(jnp.int32)
    inv_all = lax.all_to_all(
        jnp.broadcast_to(inv_root[None, :], (peer_count, rows_dev)), AXES, split_axis=0, concat_axis=0, tiled=True
    )
    terms = mirror_terms(tiles, jnp.clip(tile_row, 0, block_count - 1), live_i, scaled_t)
    terms, inv_all = lax.optimization_barrier((terms, inv_all))
    got_terms = lax.all_to_all(terms, AXES, split_axis=0, concat_axis=0, tiled=True)

    scaled_all_t = (inv_all[:, None, :] * vec_all.astype(jnp.float32)).astype(jnp.bfloat16)
    place = jnp.arange(slot_total, dtype=jnp.int32) // slot_count
    row_idx = jnp.clip(tile_row, 0, block_count - 1)
    col_idx = jnp.clip(tile_col, 0, block_count - 1)
    forward = forward_product(tiles, place, col_idx, row_idx, live_i, scaled_all_t, block_count)
    forward, got_terms = lax.optimization_barrier((forward, got_terms))
    got_hot = (got_cols[:, None] == block_ids).astype(jnp.bfloat16)
    mirror = jnp.einsum("tr,tka->rka", got_hot, got_terms, preferred_element_type=jnp.float32)
    total_t = (forward + mirror).transpose(1, 0, 2).reshape(vec_width, rows_dev)

    image_t = inv_root[None, :] * (total_t + scaled_t.astype(jnp.float32))
    local_gram = jnp.dot(image_t, image_t.T, precision=highest)
    gram = butterfly_sum(local_gram, peer_count) / jnp.float32(rows_dev * peer_count)
    lower = jnp.linalg.cholesky(gram)
    basis = jax.scipy.linalg.solve_triangular(lower, image_t, lower=True).T
    return (basis, degree)


def solution(mesh):
    placed = (
        P(AXES, None, None),
        P(AXES),
        P(AXES),
        P(AXES),
        P(AXES, None),
    )
    return jax.shard_map(
        shards,
        mesh=mesh,
        in_specs=placed,
        out_specs=(P(AXES, None), P(AXES)),
        check_vma=False,
    )
```

```python
import jax
import jax.numpy as jnp
from jax import lax
from jax.sharding import PartitionSpec as P
from jax.experimental import pallas as pl
from jax.experimental.pallas import tpu as pltpu

AXES = ("outer", "inner")


def butterfly_sum(x, peer_count):
    step = 1
    while step < peer_count:
        x = x + lax.ppermute(x, AXES, [(i, i ^ step) for i in range(peer_count)])
        step *= 2
    return x


GROUP = 32


def terms_kernel(rows_ref, live_ref, tiles_ref, own_ref, out_ref):
    step = pl.program_id(0)
    size = tiles_ref.shape[1]

    def body(j, carry):
        t = step * GROUP + j
        start = pl.multiple_of(rows_ref[t] * size, size)
        block = own_ref[:, pl.ds(start, size)]
        term = jnp.dot(block, tiles_ref[j], preferred_element_type=jnp.float32).astype(out_ref.dtype)
        out_ref[j] = jnp.where(live_ref[t] > 0, term, jnp.zeros_like(term))
        return carry

    lax.fori_loop(0, GROUP, body, 0, unroll=True)


def mirror_terms(tiles, rows, live, own_t):
    slots, size, _ = tiles.shape
    width = own_t.shape[0]
    return pl.pallas_call(
        terms_kernel,
        grid_spec=pltpu.PrefetchScalarGridSpec(
            num_scalar_prefetch=2,
            grid=(slots // GROUP,),
            in_specs=[
                pl.BlockSpec((GROUP, size, size), lambda i, r, l: (i, 0, 0)),
                pl.BlockSpec(memory_space=pltpu.VMEM),
            ],
            out_specs=pl.BlockSpec((GROUP, width, size), lambda i, r, l: (i, 0, 0)),
        ),
        out_shape=jax.ShapeDtypeStruct((slots, width, size), jnp.bfloat16),
    )(rows, live, tiles, own_t)


def forward_kernel(places_ref, cols_ref, rows_ref, live_ref, tiles_ref, all_ref, out_ref):
    step = pl.program_id(0)
    size = tiles_ref.shape[1]

    @pl.when(step == 0)
    def _():
        out_ref[...] = jnp.zeros_like(out_ref)

    def body(j, carry):
        t = step * GROUP + j
        start = pl.multiple_of(cols_ref[t] * size, size)
        block = all_ref[places_ref[t], :, pl.ds(start, size)]
        prod = lax.dot_general(
            block, tiles_ref[j], (((1,), (1,)), ((), ())), preferred_element_type=jnp.float32
        )
        r = rows_ref[t]
        out_ref[r] += jnp.where(live_ref[t] > 0, prod, jnp.zeros_like(prod))
        return carry

    lax.fori_loop(0, GROUP, body, 0, unroll=True)


def forward_product(tiles, places, cols, rows, live, scaled_all_t, block_count):
    slots, size, _ = tiles.shape
    width = scaled_all_t.shape[1]
    return pl.pallas_call(
        forward_kernel,
        grid_spec=pltpu.PrefetchScalarGridSpec(
            num_scalar_prefetch=4,
            grid=(slots // GROUP,),
            in_specs=[
                pl.BlockSpec((GROUP, size, size), lambda i, p, c, r, l: (i, 0, 0)),
                pl.BlockSpec(memory_space=pltpu.VMEM),
            ],
            out_specs=pl.BlockSpec((block_count, width, size), lambda i, p, c, r, l: (0, 0, 0)),
        ),
        out_shape=jax.ShapeDtypeStruct((block_count, width, size), jnp.float32),
    )(places, cols, rows, live, tiles, scaled_all_t)


def shards(tiles, tile_row, tile_col, counts, vectors):
    peer_count = lax.axis_size(AXES)
    outer_count = lax.axis_size("outer")
    inner_count = lax.axis_size("inner")
    slot_total = tiles.shape[0]
    slot_count = slot_total // peer_count
    tile_size = tiles.shape[1]
    rows_dev = vectors.shape[0]
    block_count = rows_dev // tile_size
    vec_width = vectors.shape[1]
    highest = lax.Precision.HIGHEST

    vec_t = vectors.T
    vec_all = lax.all_gather(vec_t, AXES, axis=0)

    slot_number = jnp.arange(slot_total, dtype=jnp.int32) % slot_count
    live = slot_number < jnp.repeat(counts, slot_count)
    block_ids = jnp.arange(block_count, dtype=jnp.int32)[None, :]
    row_hot = (tile_row[:, None] == block_ids) & live[:, None]
    col_hot = (tile_col[:, None] == block_ids) & live[:, None]

    row_sums = jnp.sum(tiles, axis=2, dtype=jnp.float32)
    col_sums = jnp.sum(tiles, axis=1, dtype=jnp.float32)
    own_part = jnp.einsum("tr,ta->ra", row_hot.astype(jnp.float32), row_sums, precision=highest)
    col_part = jnp.einsum(
        "htr,hta->hra",
        col_hot.astype(jnp.float32).reshape(peer_count, slot_count, block_count),
        col_sums.reshape(peer_count, slot_count, tile_size),
        precision=highest,
    ).reshape(peer_count, block_count * tile_size)
    got = lax.all_to_all(col_part, AXES, split_axis=0, concat_axis=0, tiled=True)
    degree_blocks = own_part + jnp.sum(got, axis=0).reshape(block_count, tile_size)

    degree = 1.0 + degree_blocks.reshape(rows_dev)
    inv_root = lax.rsqrt(degree)
    scaled = (inv_root[:, None] * vectors.astype(jnp.float32)).astype(jnp.bfloat16)

    scaled_t = scaled.T
    live_i = live.astype(jnp.int32)
    inv_payload = jnp.concatenate(
        [
            jnp.broadcast_to(inv_root[None, :], (peer_count, rows_dev)),
            tile_col.reshape(peer_count, slot_count).astype(jnp.float32),
        ],
        axis=1,
    )
    inv_got = lax.all_to_all(inv_payload, AXES, split_axis=0, concat_axis=0, tiled=True)
    inv_all = inv_got[:, :rows_dev]
    got_cols = inv_got[:, rows_dev:].astype(jnp.int32).reshape(peer_count * slot_count)
    terms = mirror_terms(tiles, tile_row, live_i, scaled_t)
    terms, inv_all = lax.optimization_barrier((terms, inv_all))
    got_terms = lax.all_to_all(terms, AXES, split_axis=0, concat_axis=0, tiled=True)

    scaled_all_t = (inv_all[:, None, :] * vec_all.astype(jnp.float32)).astype(jnp.bfloat16)
    place = jnp.arange(slot_total, dtype=jnp.int32) // slot_count
    forward = forward_product(tiles, place, tile_col, tile_row, live_i, scaled_all_t, block_count)
    forward, got_terms = lax.optimization_barrier((forward, got_terms))
    got_hot = (got_cols[:, None] == block_ids).astype(jnp.bfloat16)
    mirror = jnp.einsum("tr,tka->rka", got_hot, got_terms, preferred_element_type=jnp.float32)
    total_t = (forward + mirror).transpose(1, 0, 2).reshape(vec_width, rows_dev)

    image_t = inv_root[None, :] * (total_t + scaled_t.astype(jnp.float32))
    local_gram = jnp.dot(image_t, image_t.T, precision=highest)
    gram = butterfly_sum(local_gram, peer_count) / jnp.float32(rows_dev * peer_count)
    lower = jnp.linalg.cholesky(gram)
    basis = jax.scipy.linalg.solve_triangular(lower, image_t, lower=True).T
    return (basis, degree)


def solution(mesh):
    placed = (
        P(AXES, None, None),
        P(AXES),
        P(AXES),
        P(AXES),
        P(AXES, None),
    )
    return jax.shard_map(
        shards,
        mesh=mesh,
        in_specs=placed,
        out_specs=(P(AXES, None), P(AXES)),
        check_vma=False,
    )
```

```python
import jax
import jax.numpy as jnp
from jax import lax
from jax.sharding import PartitionSpec as P
from jax.experimental import pallas as pl
from jax.experimental.pallas import tpu as pltpu

AXES = ("outer", "inner")


def butterfly_sum(x, peer_count):
    step = 1
    while step < peer_count:
        if step * 4 <= peer_count:
            near = lax.ppermute(x, AXES, [(i, i ^ step) for i in range(peer_count)])
            far = lax.ppermute(x, AXES, [(i, i ^ (2 * step)) for i in range(peer_count)])
            far_near = lax.ppermute(x, AXES, [(i, i ^ (3 * step)) for i in range(peer_count)])
            x = (x + near) + (far + far_near)
            step *= 4
        else:
            x = x + lax.ppermute(x, AXES, [(i, i ^ step) for i in range(peer_count)])
            step *= 2
    return x


GROUP = 32


def terms_kernel(rows_ref, live_ref, tiles_ref, own_ref, out_ref):
    step = pl.program_id(0)
    size = tiles_ref.shape[1]

    def body(j, carry):
        t = step * GROUP + j
        start = pl.multiple_of(rows_ref[t] * size, size)
        block = own_ref[:, pl.ds(start, size)]
        term = jnp.dot(block, tiles_ref[j], preferred_element_type=jnp.float32).astype(out_ref.dtype)
        out_ref[j] = jnp.where(live_ref[t] > 0, term, jnp.zeros_like(term))
        return carry

    lax.fori_loop(0, GROUP, body, 0, unroll=True)


def mirror_terms(tiles, rows, live, own_t):
    slots, size, _ = tiles.shape
    width = own_t.shape[0]
    return pl.pallas_call(
        terms_kernel,
        grid_spec=pltpu.PrefetchScalarGridSpec(
            num_scalar_prefetch=2,
            grid=(slots // GROUP,),
            in_specs=[
                pl.BlockSpec((GROUP, size, size), lambda i, r, l: (i, 0, 0)),
                pl.BlockSpec(memory_space=pltpu.VMEM),
            ],
            out_specs=pl.BlockSpec((GROUP, width, size), lambda i, r, l: (i, 0, 0)),
        ),
        out_shape=jax.ShapeDtypeStruct((slots, width, size), jnp.bfloat16),
    )(rows, live, tiles, own_t)


FORWARD_GROUP = 128


def forward_kernel(places_ref, cols_ref, rows_ref, live_ref, tiles_ref, vec_ref, inv_ref, out_ref):
    step = pl.program_id(0)
    size = tiles_ref.shape[1]

    @pl.when(step == 0)
    def _():
        out_ref[...] = jnp.zeros_like(out_ref)

    for j in range(FORWARD_GROUP):
        t = step * FORWARD_GROUP + j
        p = places_ref[t]
        start = pl.multiple_of(cols_ref[t] * size, size)
        scale = inv_ref[p, :, pl.ds(start, size)]
        block = (vec_ref[p, :, pl.ds(start, size)].astype(jnp.float32) * scale).astype(tiles_ref.dtype)
        prod = lax.dot_general(
            block, tiles_ref[j], (((1,), (1,)), ((), ())), preferred_element_type=jnp.float32
        )
        r = rows_ref[t]
        out_ref[r] += jnp.where(live_ref[t] > 0, prod, jnp.zeros_like(prod))


def forward_product(tiles, places, cols, rows, live, vec_all, inv_all, block_count):
    slots, size, _ = tiles.shape
    width = vec_all.shape[1]
    return pl.pallas_call(
        forward_kernel,
        grid_spec=pltpu.PrefetchScalarGridSpec(
            num_scalar_prefetch=4,
            grid=(slots // FORWARD_GROUP,),
            in_specs=[
                pl.BlockSpec((FORWARD_GROUP, size, size), lambda i, p, c, r, l: (i, 0, 0)),
                pl.BlockSpec(memory_space=pltpu.VMEM),
                pl.BlockSpec(memory_space=pltpu.VMEM),
            ],
            out_specs=pl.BlockSpec((block_count, width, size), lambda i, p, c, r, l: (0, 0, 0)),
        ),
        out_shape=jax.ShapeDtypeStruct((block_count, width, size), jnp.float32),
    )(places, cols, rows, live, tiles, vec_all, inv_all)


def shards(tiles, tile_row, tile_col, counts, vectors):
    peer_count = lax.axis_size(AXES)
    outer_count = lax.axis_size("outer")
    inner_count = lax.axis_size("inner")
    slot_total = tiles.shape[0]
    slot_count = slot_total // peer_count
    tile_size = tiles.shape[1]
    rows_dev = vectors.shape[0]
    block_count = rows_dev // tile_size
    vec_width = vectors.shape[1]
    highest = lax.Precision.HIGHEST

    vec_t = vectors.T
    vec_all = lax.all_gather(vec_t, AXES, axis=0)

    slot_number = jnp.arange(slot_total, dtype=jnp.int32) % slot_count
    live = slot_number < jnp.repeat(counts, slot_count)
    block_ids = jnp.arange(block_count, dtype=jnp.int32)[None, :]
    row_hot = (tile_row[:, None] == block_ids) & live[:, None]
    col_hot = (tile_col[:, None] == block_ids) & live[:, None]

    row_sums = jnp.sum(tiles, axis=2, dtype=jnp.float32)
    col_sums = jnp.sum(tiles, axis=1, dtype=jnp.float32)
    own_part = jnp.einsum("tr,ta->ra", row_hot.astype(jnp.float32), row_sums, precision=highest)
    col_part = jnp.einsum(
        "htr,hta->hra",
        col_hot.astype(jnp.float32).reshape(peer_count, slot_count, block_count),
        col_sums.reshape(peer_count, slot_count, tile_size),
        precision=highest,
    ).reshape(peer_count, block_count * tile_size)
    payload = jnp.concatenate(
        [col_part, tile_col.reshape(peer_count, slot_count).astype(jnp.float32)], axis=1
    )
    got = lax.all_to_all(payload, AXES, split_axis=0, concat_axis=0, tiled=True)
    degree_blocks = own_part + jnp.sum(got[:, : block_count * tile_size], axis=0).reshape(block_count, tile_size)
    got_cols = got[:, block_count * tile_size :].astype(jnp.int32).reshape(peer_count * slot_count)

    degree = 1.0 + degree_blocks.reshape(rows_dev)
    inv_root = lax.rsqrt(degree)
    scaled = (inv_root[:, None] * vectors.astype(jnp.float32)).astype(jnp.bfloat16)

    scaled_t = scaled.T
    live_i = live.astype(jnp.int32)
    inv_all = lax.all_to_all(
        jnp.broadcast_to(inv_root[None, :], (peer_count, rows_dev)), AXES, split_axis=0, concat_axis=0, tiled=True
    )
    terms = mirror_terms(tiles, tile_row, live_i, scaled_t)
    terms, inv_all = lax.optimization_barrier((terms, inv_all))
    got_terms = lax.all_to_all(terms, AXES, split_axis=0, concat_axis=0, tiled=True)

    place = jnp.arange(slot_total, dtype=jnp.int32) // slot_count
    forward = forward_product(
        tiles, place, tile_col, tile_row, live_i, vec_all, inv_all.reshape(peer_count, 1, rows_dev), block_count
    )
    forward, got_terms = lax.optimization_barrier((forward, got_terms))
    got_hot = (got_cols[:, None] == block_ids).astype(jnp.bfloat16)
    mirror = jnp.einsum("tr,tka->rka", got_hot, got_terms, preferred_element_type=jnp.float32)
    total_t = (forward + mirror).transpose(1, 0, 2).reshape(vec_width, rows_dev)

    image_t = inv_root[None, :] * (total_t + scaled_t.astype(jnp.float32))
    local_gram = jnp.dot(image_t, image_t.T, precision=highest)
    gram = butterfly_sum(local_gram, peer_count) / jnp.float32(rows_dev * peer_count)
    lower = jnp.linalg.cholesky(gram)
    basis = jax.scipy.linalg.solve_triangular(lower, image_t, lower=True).T
    return (basis, degree)


def solution(mesh):
    placed = (
        P(AXES, None, None),
        P(AXES),
        P(AXES),
        P(AXES),
        P(AXES, None),
    )
    return jax.shard_map(
        shards,
        mesh=mesh,
        in_specs=placed,
        out_specs=(P(AXES, None), P(AXES)),
        check_vma=False,
    )
```

```python
import jax
import jax.numpy as jnp
from jax import lax
from jax.sharding import PartitionSpec as P
from jax.experimental import pallas as pl
from jax.experimental.pallas import tpu as pltpu

AXES = ("outer", "inner")


def butterfly_sum(x, peer_count):
    step = 1
    while step < peer_count:
        if step * 4 <= peer_count:
            near = lax.ppermute(x, AXES, [(i, i ^ step) for i in range(peer_count)])
            far = lax.ppermute(x, AXES, [(i, i ^ (2 * step)) for i in range(peer_count)])
            far_near = lax.ppermute(x, AXES, [(i, i ^ (3 * step)) for i in range(peer_count)])
            x = (x + near) + (far + far_near)
            step *= 4
        else:
            x = x + lax.ppermute(x, AXES, [(i, i ^ step) for i in range(peer_count)])
            step *= 2
    return x


TERMS_GROUP = 256


def terms_kernel(rows_ref, live_ref, tiles_ref, own_ref, out_ref):
    step = pl.program_id(0)
    size = tiles_ref.shape[1]

    for j in range(TERMS_GROUP):
        t = step * TERMS_GROUP + j
        start = pl.multiple_of(rows_ref[t] * size, size)
        block = own_ref[:, pl.ds(start, size)]
        term = jnp.dot(block, tiles_ref[j], preferred_element_type=jnp.float32).astype(out_ref.dtype)
        out_ref[j] = jnp.where(live_ref[t] > 0, term, jnp.zeros_like(term))


def mirror_terms(tiles, rows, live, own_t):
    slots, size, _ = tiles.shape
    width = own_t.shape[0]
    return pl.pallas_call(
        terms_kernel,
        grid_spec=pltpu.PrefetchScalarGridSpec(
            num_scalar_prefetch=2,
            grid=(slots // TERMS_GROUP,),
            in_specs=[
                pl.BlockSpec((TERMS_GROUP, size, size), lambda i, r, l: (i, 0, 0)),
                pl.BlockSpec(memory_space=pltpu.VMEM),
            ],
            out_specs=pl.BlockSpec((TERMS_GROUP, width, size), lambda i, r, l: (i, 0, 0)),
        ),
        out_shape=jax.ShapeDtypeStruct((slots, width, size), jnp.bfloat16),
    )(rows, live, tiles, own_t)


FORWARD_GROUP = 128


def forward_kernel(places_ref, cols_ref, rows_ref, live_ref, tiles_ref, vec_ref, inv_ref, out_ref):
    step = pl.program_id(0)
    size = tiles_ref.shape[1]

    @pl.when(step == 0)
    def _():
        out_ref[...] = jnp.zeros_like(out_ref)

    for j in range(FORWARD_GROUP):
        t = step * FORWARD_GROUP + j
        p = places_ref[t]
        start = pl.multiple_of(cols_ref[t] * size, size)
        scale = inv_ref[p, :, pl.ds(start, size)]
        block = (vec_ref[p, :, pl.ds(start, size)].astype(jnp.float32) * scale).astype(tiles_ref.dtype)
        prod = lax.dot_general(
            block, tiles_ref[j], (((1,), (1,)), ((), ())), preferred_element_type=jnp.float32
        )
        r = rows_ref[t]
        out_ref[r] += jnp.where(live_ref[t] > 0, prod, jnp.zeros_like(prod))


def forward_product(tiles, places, cols, rows, live, vec_all, inv_all, block_count):
    slots, size, _ = tiles.shape
    width = vec_all.shape[1]
    return pl.pallas_call(
        forward_kernel,
        grid_spec=pltpu.PrefetchScalarGridSpec(
            num_scalar_prefetch=4,
            grid=(slots // FORWARD_GROUP,),
            in_specs=[
                pl.BlockSpec((FORWARD_GROUP, size, size), lambda i, p, c, r, l: (i, 0, 0)),
                pl.BlockSpec(memory_space=pltpu.VMEM),
                pl.BlockSpec(memory_space=pltpu.VMEM),
            ],
            out_specs=pl.BlockSpec((block_count, width, size), lambda i, p, c, r, l: (0, 0, 0)),
        ),
        out_shape=jax.ShapeDtypeStruct((block_count, width, size), jnp.float32),
    )(places, cols, rows, live, tiles, vec_all, inv_all)


def shards(tiles, tile_row, tile_col, counts, vectors):
    peer_count = lax.axis_size(AXES)
    outer_count = lax.axis_size("outer")
    inner_count = lax.axis_size("inner")
    slot_total = tiles.shape[0]
    slot_count = slot_total // peer_count
    tile_size = tiles.shape[1]
    rows_dev = vectors.shape[0]
    block_count = rows_dev // tile_size
    vec_width = vectors.shape[1]
    highest = lax.Precision.HIGHEST

    vec_t = vectors.T
    vec_all = lax.all_gather(vec_t, AXES, axis=0)

    slot_number = jnp.arange(slot_total, dtype=jnp.int32) % slot_count
    live = slot_number < jnp.repeat(counts, slot_count)
    block_ids = jnp.arange(block_count, dtype=jnp.int32)[None, :]
    row_hot = (tile_row[:, None] == block_ids) & live[:, None]
    col_hot = (tile_col[:, None] == block_ids) & live[:, None]

    row_sums = jnp.sum(tiles, axis=2, dtype=jnp.float32)
    col_sums = jnp.sum(tiles, axis=1, dtype=jnp.float32)
    own_part = jnp.einsum("tr,ta->ra", row_hot.astype(jnp.float32), row_sums, precision=highest)
    col_part = jnp.einsum(
        "htr,hta->hra",
        col_hot.astype(jnp.float32).reshape(peer_count, slot_count, block_count),
        col_sums.reshape(peer_count, slot_count, tile_size),
        precision=highest,
    ).reshape(peer_count, block_count * tile_size)
    payload = jnp.concatenate(
        [col_part, tile_col.reshape(peer_count, slot_count).astype(jnp.float32)], axis=1
    )
    got = lax.all_to_all(payload, AXES, split_axis=0, concat_axis=0, tiled=True)
    degree_blocks = own_part + jnp.sum(got[:, : block_count * tile_size], axis=0).reshape(block_count, tile_size)
    got_cols = got[:, block_count * tile_size :].astype(jnp.int32).reshape(peer_count * slot_count)

    degree = 1.0 + degree_blocks.reshape(rows_dev)
    inv_root = lax.rsqrt(degree)
    scaled = (inv_root[:, None] * vectors.astype(jnp.float32)).astype(jnp.bfloat16)

    scaled_t = scaled.T
    live_i = live.astype(jnp.int32)
    inv_all = lax.all_to_all(
        jnp.broadcast_to(inv_root[None, :], (peer_count, rows_dev)), AXES, split_axis=0, concat_axis=0, tiled=True
    )
    terms = mirror_terms(tiles, tile_row, live_i, scaled_t)
    terms, inv_all = lax.optimization_barrier((terms, inv_all))
    got_terms = lax.all_to_all(terms, AXES, split_axis=0, concat_axis=0, tiled=True)

    place = jnp.arange(slot_total, dtype=jnp.int32) // slot_count
    forward = forward_product(
        tiles, place, tile_col, tile_row, live_i, vec_all, inv_all.reshape(peer_count, 1, rows_dev), block_count
    )
    forward, got_terms = lax.optimization_barrier((forward, got_terms))
    got_hot = (got_cols[:, None] == block_ids).astype(jnp.bfloat16)
    mirror = jnp.einsum("tr,tka->rka", got_hot, got_terms, preferred_element_type=jnp.float32)
    total_t = (forward + mirror).transpose(1, 0, 2).reshape(vec_width, rows_dev)

    image_t = inv_root[None, :] * (total_t + scaled_t.astype(jnp.float32))
    local_gram = jnp.dot(image_t, image_t.T, precision=highest)
    gram = butterfly_sum(local_gram, peer_count) / jnp.float32(rows_dev * peer_count)
    lower = jnp.linalg.cholesky(gram)
    basis = jax.scipy.linalg.solve_triangular(lower, image_t, lower=True).T
    return (basis, degree)


def solution(mesh):
    placed = (
        P(AXES, None, None),
        P(AXES),
        P(AXES),
        P(AXES),
        P(AXES, None),
    )
    return jax.shard_map(
        shards,
        mesh=mesh,
        in_specs=placed,
        out_specs=(P(AXES, None), P(AXES)),
        check_vma=False,
    )
```

```python
import jax
import jax.numpy as jnp
from jax import lax
from jax.sharding import PartitionSpec as P
from jax.experimental import pallas as pl
from jax.experimental.pallas import tpu as pltpu

AXES = ("outer", "inner")


def butterfly_sum(x, peer_count):
    step = 1
    while step < peer_count:
        if step * 4 <= peer_count:
            near = lax.ppermute(x, AXES, [(i, i ^ step) for i in range(peer_count)])
            far = lax.ppermute(x, AXES, [(i, i ^ (2 * step)) for i in range(peer_count)])
            far_near = lax.ppermute(x, AXES, [(i, i ^ (3 * step)) for i in range(peer_count)])
            x = (x + near) + (far + far_near)
            step *= 4
        else:
            x = x + lax.ppermute(x, AXES, [(i, i ^ step) for i in range(peer_count)])
            step *= 2
    return x


GROUP = 32


def terms_kernel(rows_ref, live_ref, tiles_ref, own_ref, out_ref):
    step = pl.program_id(0)
    size = tiles_ref.shape[1]

    def body(j, carry):
        t = step * GROUP + j
        start = pl.multiple_of(rows_ref[t] * size, size)
        block = own_ref[:, pl.ds(start, size)]
        term = jnp.dot(block, tiles_ref[j], preferred_element_type=jnp.float32).astype(out_ref.dtype)
        out_ref[j] = jnp.where(live_ref[t] > 0, term, jnp.zeros_like(term))
        return carry

    lax.fori_loop(0, GROUP, body, 0, unroll=True)


def mirror_terms(tiles, rows, live, own_t):
    slots, size, _ = tiles.shape
    width = own_t.shape[0]
    return pl.pallas_call(
        terms_kernel,
        grid_spec=pltpu.PrefetchScalarGridSpec(
            num_scalar_prefetch=2,
            grid=(slots // GROUP,),
            in_specs=[
                pl.BlockSpec((GROUP, size, size), lambda i, r, l: (i, 0, 0)),
                pl.BlockSpec(memory_space=pltpu.VMEM),
            ],
            out_specs=pl.BlockSpec((GROUP, width, size), lambda i, r, l: (i, 0, 0)),
        ),
        out_shape=jax.ShapeDtypeStruct((slots, width, size), jnp.bfloat16),
    )(rows, live, tiles, own_t)


FORWARD_GROUP = 128


def forward_kernel(places_ref, cols_ref, rows_ref, live_ref, tiles_ref, vec_ref, inv_ref, out_ref):
    step = pl.program_id(0)
    size = tiles_ref.shape[1]

    @pl.when(step == 0)
    def _():
        out_ref[...] = jnp.zeros_like(out_ref)

    for j in range(FORWARD_GROUP):
        t = step * FORWARD_GROUP + j
        p = places_ref[t]
        start = pl.multiple_of(cols_ref[t] * size, size)
        scale = inv_ref[p, :, pl.ds(start, size)]
        block = (vec_ref[p, :, pl.ds(start, size)].astype(jnp.float32) * scale).astype(tiles_ref.dtype)
        prod = lax.dot_general(
            block, tiles_ref[j], (((1,), (1,)), ((), ())), preferred_element_type=jnp.float32
        )
        r = rows_ref[t]
        out_ref[r] += jnp.where(live_ref[t] > 0, prod, jnp.zeros_like(prod))


def forward_product(tiles, places, cols, rows, live, vec_all, inv_all, block_count):
    slots, size, _ = tiles.shape
    width = vec_all.shape[1]
    return pl.pallas_call(
        forward_kernel,
        grid_spec=pltpu.PrefetchScalarGridSpec(
            num_scalar_prefetch=4,
            grid=(slots // FORWARD_GROUP,),
            in_specs=[
                pl.BlockSpec((FORWARD_GROUP, size, size), lambda i, p, c, r, l: (i, 0, 0)),
                pl.BlockSpec(memory_space=pltpu.VMEM),
                pl.BlockSpec(memory_space=pltpu.VMEM),
            ],
            out_specs=pl.BlockSpec((block_count, width, size), lambda i, p, c, r, l: (0, 0, 0)),
        ),
        out_shape=jax.ShapeDtypeStruct((block_count, width, size), jnp.float32),
    )(places, cols, rows, live, tiles, vec_all, inv_all)


def shards(tiles, tile_row, tile_col, counts, vectors):
    peer_count = lax.axis_size(AXES)
    outer_count = lax.axis_size("outer")
    inner_count = lax.axis_size("inner")
    slot_total = tiles.shape[0]
    slot_count = slot_total // peer_count
    tile_size = tiles.shape[1]
    rows_dev = vectors.shape[0]
    block_count = rows_dev // tile_size
    vec_width = vectors.shape[1]
    highest = lax.Precision.HIGHEST

    vec_t = vectors.T
    outer_me = lax.axis_index("outer")
    shifted = [vec_t] + [
        lax.ppermute(vec_t, "outer", [(i, (i + k) % outer_count) for i in range(outer_count)])
        for k in range(1, outer_count)
    ]
    vec_all = lax.all_gather(jnp.stack(shifted), "inner", axis=0)
    vec_all = vec_all.reshape(peer_count, vec_width, rows_dev)

    slot_number = jnp.arange(slot_total, dtype=jnp.int32) % slot_count
    live = slot_number < jnp.repeat(counts, slot_count)
    block_ids = jnp.arange(block_count, dtype=jnp.int32)[None, :]
    row_hot = (tile_row[:, None] == block_ids) & live[:, None]
    col_hot = (tile_col[:, None] == block_ids) & live[:, None]

    row_sums = jnp.sum(tiles, axis=2, dtype=jnp.float32)
    col_sums = jnp.sum(tiles, axis=1, dtype=jnp.float32)
    own_part = jnp.einsum("tr,ta->ra", row_hot.astype(jnp.float32), row_sums, precision=highest)
    col_part = jnp.einsum(
        "htr,hta->hra",
        col_hot.astype(jnp.float32).reshape(peer_count, slot_count, block_count),
        col_sums.reshape(peer_count, slot_count, tile_size),
        precision=highest,
    ).reshape(peer_count, block_count * tile_size)
    payload = jnp.concatenate(
        [col_part, tile_col.reshape(peer_count, slot_count).astype(jnp.float32)], axis=1
    )
    got = lax.all_to_all(payload, AXES, split_axis=0, concat_axis=0, tiled=True)
    degree_blocks = own_part + jnp.sum(got[:, : block_count * tile_size], axis=0).reshape(block_count, tile_size)
    got_cols = got[:, block_count * tile_size :].astype(jnp.int32).reshape(peer_count * slot_count)

    degree = 1.0 + degree_blocks.reshape(rows_dev)
    inv_root = lax.rsqrt(degree)
    scaled = (inv_root[:, None] * vectors.astype(jnp.float32)).astype(jnp.bfloat16)

    scaled_t = scaled.T
    live_i = live.astype(jnp.int32)
    inv_all = lax.all_to_all(
        jnp.broadcast_to(inv_root[None, :], (peer_count, rows_dev)), AXES, split_axis=0, concat_axis=0, tiled=True
    )
    terms = mirror_terms(tiles, tile_row, live_i, scaled_t)
    terms, inv_all = lax.optimization_barrier((terms, inv_all))
    got_terms = lax.all_to_all(terms, AXES, split_axis=0, concat_axis=0, tiled=True)

    dest = jnp.arange(slot_total, dtype=jnp.int32) // slot_count
    place = (dest % inner_count) * outer_count + (outer_me - dest // inner_count) % outer_count
    held = jnp.arange(peer_count, dtype=jnp.int32)
    source = ((outer_me - held % outer_count) % outer_count) * inner_count + held // outer_count
    inv_held = inv_all[source].reshape(peer_count, 1, rows_dev)
    forward = forward_product(tiles, place, tile_col, tile_row, live_i, vec_all, inv_held, block_count)
    forward, got_terms = lax.optimization_barrier((forward, got_terms))
    got_hot = (got_cols[:, None] == block_ids).astype(jnp.bfloat16)
    mirror = jnp.einsum("tr,tka->rka", got_hot, got_terms, preferred_element_type=jnp.float32)
    total_t = (forward + mirror).transpose(1, 0, 2).reshape(vec_width, rows_dev)

    image_t = inv_root[None, :] * (total_t + scaled_t.astype(jnp.float32))
    local_gram = jnp.dot(image_t, image_t.T, precision=highest)
    gram = butterfly_sum(local_gram, peer_count) / jnp.float32(rows_dev * peer_count)
    lower = jnp.linalg.cholesky(gram)
    basis = jax.scipy.linalg.solve_triangular(lower, image_t, lower=True).T
    return (basis, degree)


def solution(mesh):
    placed = (
        P(AXES, None, None),
        P(AXES),
        P(AXES),
        P(AXES),
        P(AXES, None),
    )
    return jax.shard_map(
        shards,
        mesh=mesh,
        in_specs=placed,
        out_specs=(P(AXES, None), P(AXES)),
        check_vma=False,
    )
```

```python
import jax
import jax.numpy as jnp
from jax import lax
from jax.sharding import PartitionSpec as P
from jax.experimental import pallas as pl
from jax.experimental.pallas import tpu as pltpu

AXES = ("outer", "inner")


def butterfly_sum(x, peer_count):
    step = 1
    while step < peer_count:
        if step * 4 <= peer_count:
            near = lax.ppermute(x, AXES, [(i, i ^ step) for i in range(peer_count)])
            far = lax.ppermute(x, AXES, [(i, i ^ (2 * step)) for i in range(peer_count)])
            far_near = lax.ppermute(x, AXES, [(i, i ^ (3 * step)) for i in range(peer_count)])
            x = (x + near) + (far + far_near)
            step *= 4
        else:
            x = x + lax.ppermute(x, AXES, [(i, i ^ step) for i in range(peer_count)])
            step *= 2
    return x


GROUP = 32


def terms_kernel(rows_ref, live_ref, tiles_ref, own_ref, out_ref):
    step = pl.program_id(0)
    size = tiles_ref.shape[1]

    def body(j, carry):
        t = step * GROUP + j
        start = pl.multiple_of(rows_ref[t] * size, size)
        block = own_ref[:, pl.ds(start, size)]
        term = jnp.dot(block, tiles_ref[j], preferred_element_type=jnp.float32).astype(out_ref.dtype)
        out_ref[j] = jnp.where(live_ref[t] > 0, term, jnp.zeros_like(term))
        return carry

    lax.fori_loop(0, GROUP, body, 0, unroll=True)


def mirror_terms(tiles, rows, live, own_t):
    slots, size, _ = tiles.shape
    width = own_t.shape[0]
    return pl.pallas_call(
        terms_kernel,
        grid_spec=pltpu.PrefetchScalarGridSpec(
            num_scalar_prefetch=2,
            grid=(slots // GROUP,),
            in_specs=[
                pl.BlockSpec((GROUP, size, size), lambda i, r, l: (i, 0, 0)),
                pl.BlockSpec(memory_space=pltpu.VMEM),
            ],
            out_specs=pl.BlockSpec((GROUP, width, size), lambda i, r, l: (i, 0, 0)),
        ),
        out_shape=jax.ShapeDtypeStruct((slots, width, size), jnp.bfloat16),
    )(rows, live, tiles, own_t)


FORWARD_GROUP = 128


def forward_kernel(places_ref, cols_ref, rows_ref, live_ref, tiles_ref, vec_ref, inv_ref, out_ref):
    step = pl.program_id(0)
    size = tiles_ref.shape[1]

    @pl.when(step == 0)
    def _():
        out_ref[...] = jnp.zeros_like(out_ref)

    for j in range(FORWARD_GROUP):
        t = step * FORWARD_GROUP + j
        p = places_ref[t]
        start = pl.multiple_of(cols_ref[t] * size, size)
        scale = inv_ref[p, :, pl.ds(start, size)]
        block = (vec_ref[p, :, pl.ds(start, size)].astype(jnp.float32) * scale).astype(tiles_ref.dtype)
        prod = lax.dot_general(
            block, tiles_ref[j], (((1,), (1,)), ((), ())), preferred_element_type=jnp.float32
        )
        r = rows_ref[t]
        out_ref[r] += jnp.where(live_ref[t] > 0, prod, jnp.zeros_like(prod))


def forward_product(tiles, places, cols, rows, live, vec_all, inv_all, block_count):
    slots, size, _ = tiles.shape
    width = vec_all.shape[1]
    return pl.pallas_call(
        forward_kernel,
        grid_spec=pltpu.PrefetchScalarGridSpec(
            num_scalar_prefetch=4,
            grid=(slots // FORWARD_GROUP,),
            in_specs=[
                pl.BlockSpec((FORWARD_GROUP, size, size), lambda i, p, c, r, l: (i, 0, 0)),
                pl.BlockSpec(memory_space=pltpu.VMEM),
                pl.BlockSpec(memory_space=pltpu.VMEM),
            ],
            out_specs=pl.BlockSpec((block_count, width, size), lambda i, p, c, r, l: (0, 0, 0)),
        ),
        out_shape=jax.ShapeDtypeStruct((block_count, width, size), jnp.float32),
    )(places, cols, rows, live, tiles, vec_all, inv_all)


def shards(tiles, tile_row, tile_col, counts, vectors):
    peer_count = lax.axis_size(AXES)
    outer_count = lax.axis_size("outer")
    inner_count = lax.axis_size("inner")
    slot_total = tiles.shape[0]
    slot_count = slot_total // peer_count
    tile_size = tiles.shape[1]
    rows_dev = vectors.shape[0]
    block_count = rows_dev // tile_size
    vec_width = vectors.shape[1]
    highest = lax.Precision.HIGHEST

    vec_t = vectors.T
    vec_all = lax.all_gather(vec_t, AXES, axis=0)

    slot_number = jnp.arange(slot_total, dtype=jnp.int32) % slot_count
    live = slot_number < jnp.repeat(counts, slot_count)
    block_ids = jnp.arange(block_count, dtype=jnp.int32)[None, :]
    row_hot = (tile_row[:, None] == block_ids) & live[:, None]
    col_hot = (tile_col[:, None] == block_ids) & live[:, None]

    row_sums = jnp.sum(tiles, axis=2, dtype=jnp.float32)
    col_sums = jnp.sum(tiles, axis=1, dtype=jnp.float32)
    own_part = jnp.einsum("tr,ta->ra", row_hot.astype(jnp.float32), row_sums, precision=highest)
    col_part = jnp.einsum(
        "htr,hta->hra",
        col_hot.astype(jnp.float32).reshape(peer_count, slot_count, block_count),
        col_sums.reshape(peer_count, slot_count, tile_size),
        precision=highest,
    ).reshape(peer_count, block_count * tile_size)
    payload = jnp.concatenate(
        [col_part, tile_col.reshape(peer_count, slot_count).astype(jnp.float32)], axis=1
    )
    got = lax.all_to_all(payload, AXES, split_axis=0, concat_axis=0, tiled=True)
    degree_blocks = own_part + jnp.sum(got[:, : block_count * tile_size], axis=0).reshape(block_count, tile_size)
    got_cols = got[:, block_count * tile_size :].astype(jnp.int32).reshape(peer_count * slot_count)

    degree = 1.0 + degree_blocks.reshape(rows_dev)
    inv_root = lax.rsqrt(degree)
    scaled = (inv_root[:, None] * vectors.astype(jnp.float32)).astype(jnp.bfloat16)

    scaled_t = scaled.T
    live_i = live.astype(jnp.int32)
    inv_all = lax.all_to_all(
        jnp.broadcast_to(inv_root[None, :], (peer_count, rows_dev)), AXES, split_axis=0, concat_axis=0, tiled=True
    )
    terms = mirror_terms(tiles, tile_row, live_i, scaled_t)
    terms, inv_all = lax.optimization_barrier((terms, inv_all))
    got_terms = lax.all_to_all(terms, AXES, split_axis=0, concat_axis=0, tiled=True)

    place = jnp.arange(slot_total, dtype=jnp.int32) // slot_count
    forward = forward_product(
        tiles, place, tile_col, tile_row, live_i, vec_all, inv_all.reshape(peer_count, 1, rows_dev), block_count
    )
    forward, got_terms = lax.optimization_barrier((forward, got_terms))
    got_hot = (got_cols[:, None] == block_ids).astype(jnp.bfloat16)
    mirror = jnp.dot(
        got_hot.T, got_terms.reshape(got_terms.shape[0], -1), preferred_element_type=jnp.float32
    ).reshape(block_count, vec_width, tile_size)
    total_t = (forward + mirror).transpose(1, 0, 2).reshape(vec_width, rows_dev)

    image_t = inv_root[None, :] * (total_t + scaled_t.astype(jnp.float32))
    local_gram = jnp.dot(image_t, image_t.T, precision=highest)
    gram = butterfly_sum(local_gram, peer_count) / jnp.float32(rows_dev * peer_count)
    lower = jnp.linalg.cholesky(gram)
    basis = jax.scipy.linalg.solve_triangular(lower, image_t, lower=True).T
    return (basis, degree)


def solution(mesh):
    placed = (
        P(AXES, None, None),
        P(AXES),
        P(AXES),
        P(AXES),
        P(AXES, None),
    )
    return jax.shard_map(
        shards,
        mesh=mesh,
        in_specs=placed,
        out_specs=(P(AXES, None), P(AXES)),
        check_vma=False,
    )
```

```python
import jax
import jax.numpy as jnp
from jax import lax
from jax.sharding import PartitionSpec as P
from jax.experimental import pallas as pl
from jax.experimental.pallas import tpu as pltpu

AXES = ("outer", "inner")


def butterfly_sum(x, peer_count):
    step = 1
    while step < peer_count:
        if step * 4 <= peer_count:
            near = lax.ppermute(x, AXES, [(i, i ^ step) for i in range(peer_count)])
            far = lax.ppermute(x, AXES, [(i, i ^ (2 * step)) for i in range(peer_count)])
            far_near = lax.ppermute(x, AXES, [(i, i ^ (3 * step)) for i in range(peer_count)])
            x = (x + near) + (far + far_near)
            step *= 4
        else:
            x = x + lax.ppermute(x, AXES, [(i, i ^ step) for i in range(peer_count)])
            step *= 2
    return x


GROUP = 32


def terms_kernel(rows_ref, live_ref, tiles_ref, own_ref, out_ref):
    step = pl.program_id(0)
    size = tiles_ref.shape[1]

    def body(j, carry):
        t = step * GROUP + j
        start = pl.multiple_of(rows_ref[t] * size, size)
        block = own_ref[:, pl.ds(start, size)]
        term = jnp.dot(block, tiles_ref[j], preferred_element_type=jnp.float32).astype(out_ref.dtype)
        out_ref[j] = jnp.where(live_ref[t] > 0, term, jnp.zeros_like(term))
        return carry

    lax.fori_loop(0, GROUP, body, 0, unroll=True)


def mirror_terms(tiles, rows, live, own_t):
    slots, size, _ = tiles.shape
    width = own_t.shape[0]
    return pl.pallas_call(
        terms_kernel,
        grid_spec=pltpu.PrefetchScalarGridSpec(
            num_scalar_prefetch=2,
            grid=(slots // GROUP,),
            in_specs=[
                pl.BlockSpec((GROUP, size, size), lambda i, r, l: (i, 0, 0)),
                pl.BlockSpec(memory_space=pltpu.VMEM),
            ],
            out_specs=pl.BlockSpec((GROUP, width, size), lambda i, r, l: (i, 0, 0)),
        ),
        out_shape=jax.ShapeDtypeStruct((slots, width, size), jnp.bfloat16),
    )(rows, live, tiles, own_t)


FORWARD_GROUP = 128


def forward_kernel(places_ref, cols_ref, rows_ref, live_ref, tiles_ref, vec_ref, inv_ref, out_ref):
    step = pl.program_id(0)
    size = tiles_ref.shape[1]

    @pl.when(step == 0)
    def _():
        out_ref[...] = jnp.zeros_like(out_ref)

    for j in range(FORWARD_GROUP):
        t = step * FORWARD_GROUP + j
        p = places_ref[t]
        start = pl.multiple_of(cols_ref[t] * size, size)
        scale = inv_ref[p, :, pl.ds(start, size)]
        block = (vec_ref[p, :, pl.ds(start, size)].astype(jnp.float32) * scale).astype(tiles_ref.dtype)
        prod = lax.dot_general(
            block, tiles_ref[j], (((1,), (1,)), ((), ())), preferred_element_type=jnp.float32
        )
        r = rows_ref[t]
        out_ref[r] += jnp.where(live_ref[t] > 0, prod, jnp.zeros_like(prod))


def forward_product(tiles, places, cols, rows, live, vec_all, inv_all, block_count):
    slots, size, _ = tiles.shape
    width = vec_all.shape[1]
    return pl.pallas_call(
        forward_kernel,
        grid_spec=pltpu.PrefetchScalarGridSpec(
            num_scalar_prefetch=4,
            grid=(slots // FORWARD_GROUP,),
            in_specs=[
                pl.BlockSpec((FORWARD_GROUP, size, size), lambda i, p, c, r, l: (i, 0, 0)),
                pl.BlockSpec(memory_space=pltpu.VMEM),
                pl.BlockSpec(memory_space=pltpu.VMEM),
            ],
            out_specs=pl.BlockSpec((block_count, width, size), lambda i, p, c, r, l: (0, 0, 0)),
        ),
        out_shape=jax.ShapeDtypeStruct((block_count, width, size), jnp.float32),
    )(places, cols, rows, live, tiles, vec_all, inv_all)


def shards(tiles, tile_row, tile_col, counts, vectors):
    peer_count = lax.axis_size(AXES)
    outer_count = lax.axis_size("outer")
    inner_count = lax.axis_size("inner")
    slot_total = tiles.shape[0]
    slot_count = slot_total // peer_count
    tile_size = tiles.shape[1]
    rows_dev = vectors.shape[0]
    block_count = rows_dev // tile_size
    vec_width = vectors.shape[1]
    highest = lax.Precision.HIGHEST

    vec_t = vectors.T
    vec_all = lax.all_gather(vec_t, AXES, axis=0)

    slot_number = jnp.arange(slot_total, dtype=jnp.int32) % slot_count
    live = slot_number < jnp.repeat(counts, slot_count)
    block_ids = jnp.arange(block_count, dtype=jnp.int32)[None, :]
    row_hot = (tile_row[:, None] == block_ids) & live[:, None]
    col_hot = (tile_col[:, None] == block_ids) & live[:, None]

    row_sums = jnp.sum(tiles, axis=2, dtype=jnp.float32)
    col_sums = jnp.sum(tiles, axis=1, dtype=jnp.float32)
    own_part = jnp.einsum("tr,ta->ra", row_hot.astype(jnp.float32), row_sums, precision=highest)
    col_part = jnp.einsum(
        "htr,hta->hra",
        col_hot.astype(jnp.float32).reshape(peer_count, slot_count, block_count),
        col_sums.reshape(peer_count, slot_count, tile_size),
        precision=highest,
    ).reshape(peer_count, block_count * tile_size)
    payload = jnp.concatenate(
        [col_part, tile_col.reshape(peer_count, slot_count).astype(jnp.float32)], axis=1
    )
    got = lax.all_to_all(payload, AXES, split_axis=0, concat_axis=0, tiled=True)
    degree_blocks = own_part + jnp.sum(got[:, : block_count * tile_size], axis=0).reshape(block_count, tile_size)
    got_cols = got[:, block_count * tile_size :].astype(jnp.int32).reshape(peer_count * slot_count)

    degree = 1.0 + degree_blocks.reshape(rows_dev)
    inv_root = lax.rsqrt(degree)
    scaled = (inv_root[:, None] * vectors.astype(jnp.float32)).astype(jnp.bfloat16)

    scaled_t = scaled.T
    live_i = live.astype(jnp.int32)
    inv_all = lax.all_to_all(
        jnp.broadcast_to(inv_root[None, :], (peer_count, rows_dev)), AXES, split_axis=0, concat_axis=0, tiled=True
    )
    terms = mirror_terms(tiles, tile_row, live_i, scaled_t)
    terms, inv_all = lax.optimization_barrier((terms, inv_all))
    got_terms = lax.all_to_all(terms, AXES, split_axis=0, concat_axis=0, tiled=True)

    place = jnp.arange(slot_total, dtype=jnp.int32) // slot_count
    forward = forward_product(
        tiles, place, tile_col, tile_row, live_i, vec_all, inv_all.reshape(peer_count, 1, rows_dev), block_count
    )
    forward, got_terms = lax.optimization_barrier((forward, got_terms))
    got_hot = (got_cols[:, None] == block_ids).astype(jnp.bfloat16)
    mirror = jnp.einsum("tr,tka->rka", got_hot, got_terms, preferred_element_type=jnp.float32)
    total_t = (forward + mirror).transpose(1, 0, 2).reshape(vec_width, rows_dev)

    image_t = inv_root[None, :] * (total_t + scaled_t.astype(jnp.float32))
    local_gram = jnp.dot(image_t, image_t.T, precision=highest)
    gram = butterfly_sum(local_gram, peer_count) / jnp.float32(rows_dev * peer_count)
    lower = lax.linalg.cholesky(gram, symmetrize_input=False)
    basis = jax.scipy.linalg.solve_triangular(lower, image_t, lower=True).T
    return (basis, degree)


def solution(mesh):
    placed = (
        P(AXES, None, None),
        P(AXES),
        P(AXES),
        P(AXES),
        P(AXES, None),
    )
    return jax.shard_map(
        shards,
        mesh=mesh,
        in_specs=placed,
        out_specs=(P(AXES, None), P(AXES)),
        check_vma=False,
    )
```
